128 devices in a mesh: grp: 2 (over y_hi), row: 64 (over z, y_lo, x, core).
Axes of the slice: x: 4, y: 4 (y_hi: 2, y_lo: 2; y = y_hi * 2 + y_lo), z: 4, core: 2. Of those that a mesh axis runs over, the one named last changes fastest.
Arguments:
- features: bfloat16 [65536, 256], P(('grp', 'row')), may hold values from -6 to 6
- weight: bfloat16 [256, 256], replicated, may hold values from -0.375 to 0.375
- block_vals: bfloat16 [2, 512, 16, 128, 128], P('grp', 'row'), may hold values from -0.125 to 0.125
- block_cols: int32 [2, 512, 16], P('grp', 'row'), may hold values from 0 to 255, as said below
- block_count: int32 [2, 512], P('grp', 'row'), may hold values from 1 to 16, as said below
- cotangent: bfloat16 [65536, 256], P(('grp', 'row')), may hold values from -6 to 6
Outputs:
- activated: bfloat16 [65536, 256], P(('grp', 'row'))
- weight_grad: float32 [256, 256], replicated
- input_grad: bfloat16 [65536, 256], P(('grp', 'row'))
The draws below stay inside these ranges and needn't reach their ends.
Inputs may be any that keep to these rules, and one draw needn't show every extreme that they name: `block_cols`: within one destination row block the 16 column blocks are distinct and ascending. `block_count`: in every draw some device holds 16 live slots in each of its row blocks.
All inputs are finite; a program needn't handle non-finite values.
Results may differ from the reference program's by a relative error of at most 0.0062.
Values may be sent and summed in bfloat16 or wider, within the bound.
No kernel may reach another device: no remote copies, remote signals or barrier semaphores. Data moves between devices by JAX's collectives and lax.ppermute only.
A program may use at most 128 MiB of HBM per device.

```python
import math
import jax
import jax.numpy as jnp
from jax import lax

F = 256
BS = 128
KR = 16
V_DEV = 512
VERTS = 65536
RB_DEV = 8
ROWBLK = 512
PCB = 256
N_GRP = 2
N_ROW = 64


def draw_block_cols(key, part):
    scores = jax.random.randint(key, (N_GRP, ROWBLK, PCB), 0, 1 << 20)
    scores = scores * PCB + jnp.arange(PCB, dtype=jnp.int32)[None, None, :]
    order = jnp.argsort(scores, axis=-1)[:, :, :KR]
    return jnp.sort(order, axis=-1).astype(jnp.int32)


def draw_block_count(key, part):
    first, second, third = jax.random.split(jax.random.fold_in(key, 17), 3)
    shifts = jax.random.randint(first, (N_GRP, N_ROW, 1), 0, 4)
    levels = jax.random.randint(second, (N_GRP, N_ROW, RB_DEV), 12, 17)
    counts = jnp.right_shift(KR * levels // 16, shifts)
    counts = jnp.maximum(counts, 1)
    busiest = jax.random.randint(third, (), 0, N_GRP * N_ROW)
    device_ids = jnp.arange(N_GRP * N_ROW, dtype=jnp.int32).reshape(N_GRP, N_ROW, 1)
    counts = jnp.where(device_ids == busiest, KR, counts)
    return counts.reshape(N_GRP, N_ROW * RB_DEV).astype(jnp.int32)


def steps_of(stream_key, shape, shards, low, high):
    loudness, own = 1.0, jax.random.fold_in(stream_key, 6)
    for position, blocks in shards:
        draws = jnp.exp(jax.random.uniform(jax.random.fold_in(own, position), (blocks,), jnp.float32, low / len(shards), high / len(shards)))
        loudness = loudness * jnp.repeat(draws, shape[position] // blocks).reshape([-1 if axis == position else 1 for axis in range(len(shape))])
    return loudness


def bell_draw(stream_key, dims, scale, reach, shards=(), held_as=jnp.bfloat16):
    factor_of = steps_of(stream_key, dims, shards, -0.22, 0.18) if shards else 1.0
    result = jax.random.normal(stream_key, dims, jnp.float32) * scale * factor_of
    return jnp.minimum(jnp.maximum(result, -reach), reach).astype(held_as)


def setup_inputs(seed: int = 0) -> dict:
    streams_of = jax.random.split(jax.random.key(seed), 7)
    features = bell_draw(streams_of[0], (VERTS, F), 1.0, 6.0, ((0, 128),))
    weight = bell_draw(streams_of[1], (F, F), F ** -0.5, 0.375)
    block_vals = bell_draw(streams_of[2], (N_GRP, ROWBLK, KR, BS, BS), (KR * BS) ** -0.5, 0.125, ((0, 2), (1, 64)))
    block_cols = draw_block_cols(jax.random.fold_in(streams_of[6], 71), 0)
    block_count = draw_block_count(jax.random.fold_in(streams_of[6], 71), 0)
    cotangent = bell_draw(streams_of[5], (VERTS, F), 1.0, 6.0, ((0, 128),))
    return {"features": features, "weight": weight, "block_vals": block_vals, "block_cols": block_cols, "block_count": block_count, "cotangent": cotangent}


def silu_slope(pre):
    sigma = jax.nn.sigmoid(pre)
    return sigma * (1.0 + pre * (1.0 - sigma))

def reference(features, weight, block_vals, block_cols, block_count, cotangent):
    slots = jnp.arange(KR)
    panel_rows = N_ROW * V_DEV
    per_dev = V_DEV // BS
    partial_total = jnp.zeros((VERTS, F), jnp.float32)
    for group in range(N_GRP):
        panel_blocks = features[group * panel_rows:(group + 1) * panel_rows].reshape(PCB, BS, F)

        def aggregate(items):
            values, columns, count = items
            masked = jnp.where((slots < count)[:, None, None], values, jnp.zeros_like(values))
            picked = panel_blocks[columns]
            return jnp.einsum('kij,kjf->if', masked.astype(jnp.float32), picked.astype(jnp.float32))
        sums = lax.map(aggregate, (block_vals[group], block_cols[group], block_count[group]))
        sums = sums.reshape(N_ROW, N_GRP, per_dev, BS, F).transpose(1, 0, 2, 3, 4).reshape(VERTS, F)
        partial_total = partial_total + sums
    aggregated = partial_total.astype(jnp.bfloat16)
    pre = jnp.dot(aggregated, weight, preferred_element_type=jnp.float32)
    activated = jax.nn.silu(pre).astype(jnp.bfloat16)
    pre_grad = (cotangent.astype(jnp.float32) * silu_slope(pre)).astype(jnp.bfloat16)
    weight_grad = jnp.dot(aggregated.T, pre_grad, preferred_element_type=jnp.float32) * (1.0 / math.sqrt(VERTS))
    agg_grad = jnp.dot(pre_grad, weight.T, preferred_element_type=jnp.float32).astype(jnp.bfloat16)
    by_block = agg_grad.reshape(N_GRP, N_ROW, per_dev, BS, F).transpose(1, 0, 2, 3, 4).reshape(ROWBLK, BS, F)
    panels = []
    for group in range(N_GRP):

        def spread(carry, items):
            values, columns, count, grad_rows = items
            masked = jnp.where((slots < count)[:, None, None], values, jnp.zeros_like(values))
            contrib = jnp.einsum('kij,if->kjf', masked.astype(jnp.float32), grad_rows.astype(jnp.float32))
            return (carry.at[columns].add(contrib), None)
        total, unused = lax.scan(spread, jnp.zeros((PCB, BS, F), jnp.float32), (block_vals[group], block_cols[group], block_count[group], by_block))
        panels.append(total.reshape(PCB * BS, F))
    input_grad = jnp.concatenate(panels, axis=0).astype(jnp.bfloat16)
    return (activated, weight_grad, input_grad)
```

```python
import functools
import math

import jax
import jax.numpy as jnp
from jax import lax
from jax.experimental import pallas as pl
from jax.experimental.pallas import tpu as pltpu
from jax.sharding import PartitionSpec as P

VMEM_LIMIT = 60 * 1024 * 1024


def silu_slope(pre):
    sigma = jax.nn.sigmoid(pre)
    return sigma * (1.0 + pre * (1.0 - sigma))


def aggregate_kernel(cols_ref, count_ref, vals_hbm, panel_hbm, out_ref, vals, panel, sems):
    row_blocks, slot_total, block, _ = vals.shape
    col_blocks = panel.shape[0] // block
    load_vals = pltpu.make_async_copy(vals_hbm, vals, sems.at[0])
    load_panel = pltpu.make_async_copy(panel_hbm, panel, sems.at[1])
    load_vals.start()
    load_panel.start()
    load_vals.wait()
    load_panel.wait()
    for t in range(row_blocks):
        live = jnp.clip(count_ref[t], 0, slot_total)

        def body(k, acc):
            col = jnp.clip(cols_ref[t, k], 0, col_blocks - 1)
            start = pl.multiple_of(col * block, block)
            return acc + jnp.dot(
                vals[t, k], panel[pl.ds(start, block), :], preferred_element_type=jnp.float32
            )

        out_ref[t] = lax.fori_loop(0, live, body, jnp.zeros(out_ref.shape[1:], jnp.float32))


def spread_kernel(cols_ref, count_ref, vals_hbm, grad_ref, out_hbm, vals, total, sems):
    row_blocks, slot_total, block, _ = vals.shape
    col_blocks = total.shape[0]
    load_vals = pltpu.make_async_copy(vals_hbm, vals, sems.at[0])
    load_vals.start()

    def clear(c, carry):
        total[c] = jnp.zeros(total.shape[1:], total.dtype)
        return carry

    lax.fori_loop(0, col_blocks, clear, 0)
    load_vals.wait()
    for t in range(row_blocks):
        live = jnp.clip(count_ref[t], 0, slot_total)
        grad = grad_ref[t]

        def body(k, carry):
            col = jnp.clip(cols_ref[t, k], 0, col_blocks - 1)
            contrib = lax.dot_general(
                vals[t, k], grad, (((0,), (0,)), ((), ())), preferred_element_type=jnp.float32
            )
            total[col] += contrib
            return carry

        lax.fori_loop(0, live, body, 0)
    store = pltpu.make_async_copy(total, out_hbm, sems.at[1])
    store.start()
    store.wait()


def aggregate(cols, count, vals, panel):
    row_blocks, slot_total, block, _ = vals.shape
    width = panel.shape[1]
    return pl.pallas_call(
        aggregate_kernel,
        out_shape=jax.ShapeDtypeStruct((row_blocks, block, width), jnp.float32),
        in_specs=[
            pl.BlockSpec(memory_space=pltpu.SMEM),
            pl.BlockSpec(memory_space=pltpu.SMEM),
            pl.BlockSpec(memory_space=pl.ANY),
            pl.BlockSpec(memory_space=pl.ANY),
        ],
        out_specs=pl.BlockSpec(memory_space=pltpu.VMEM),
        scratch_shapes=[
            pltpu.VMEM(vals.shape, vals.dtype),
            pltpu.VMEM(panel.shape, panel.dtype),
            pltpu.SemaphoreType.DMA((2,)),
        ],
        compiler_params=pltpu.CompilerParams(vmem_limit_bytes=VMEM_LIMIT),
        cost_estimate=pl.CostEstimate(
            flops=2 * row_blocks * slot_total * block * block * width,
            bytes_accessed=vals.size * 2 + panel.size * 2 + row_blocks * block * width * 4,
            transcendentals=0,
        ),
    )(cols, count, vals, panel)


def spread(cols, count, vals, grad, col_blocks):
    row_blocks, slot_total, block, _ = vals.shape
    width = grad.shape[-1]
    return pl.pallas_call(
        spread_kernel,
        out_shape=jax.ShapeDtypeStruct((col_blocks, block, width), jnp.float32),
        in_specs=[
            pl.BlockSpec(memory_space=pltpu.SMEM),
            pl.BlockSpec(memory_space=pltpu.SMEM),
            pl.BlockSpec(memory_space=pl.ANY),
            pl.BlockSpec(memory_space=pltpu.VMEM),
        ],
        out_specs=pl.BlockSpec(memory_space=pl.ANY),
        scratch_shapes=[
            pltpu.VMEM(vals.shape, vals.dtype),
            pltpu.VMEM((col_blocks, block, width), jnp.float32),
            pltpu.SemaphoreType.DMA((2,)),
        ],
        compiler_params=pltpu.CompilerParams(vmem_limit_bytes=VMEM_LIMIT),
        cost_estimate=pl.CostEstimate(
            flops=2 * row_blocks * slot_total * block * block * width,
            bytes_accessed=vals.size * 2 + grad.size * 2 + col_blocks * block * width * 4,
            transcendentals=0,
        ),
    )(cols, count, vals, grad)


def body(features, weight, block_vals, block_cols, block_count, cotangent):
    rows_dev, width = features.shape
    block = block_vals.shape[-1]
    groups = lax.axis_size("grp")
    members = lax.axis_size("row")
    verts = rows_dev * groups * members
    gathered = lax.all_gather(features, "row", axis=0, tiled=True)
    col_blocks = gathered.shape[0] // block
    cols = block_cols[0]
    count = block_count[0]
    vals = block_vals[0]

    partial_value = aggregate(cols, count, vals, gathered).reshape(-1, width)
    summed = lax.psum_scatter(partial_value, "grp", scatter_dimension=0, tiled=True)
    aggregated = summed.astype(jnp.bfloat16)
    pre = jnp.dot(aggregated, weight, preferred_element_type=jnp.float32)
    activated = jax.nn.silu(pre).astype(jnp.bfloat16)
    pre_grad = (cotangent.astype(jnp.float32) * silu_slope(pre)).astype(jnp.bfloat16)
    local_grad = jnp.dot(aggregated.T, pre_grad, preferred_element_type=jnp.float32)
    own_grad = jnp.dot(pre_grad, weight.T, preferred_element_type=jnp.float32).astype(jnp.bfloat16)
    rows_grad = lax.all_gather(own_grad, "grp", axis=0, tiled=True)
    weight_grad = lax.psum(local_grad, ("grp", "row")) * (1.0 / math.sqrt(verts))
    by_block = rows_grad.reshape(-1, block, width)

    term = spread(cols, count, vals, by_block, col_blocks).reshape(-1, width)
    input_grad = lax.psum_scatter(term, "row", scatter_dimension=0, tiled=True).astype(jnp.bfloat16)
    return (activated, weight_grad, input_grad)


def solution(mesh):
    placed = (
        P(("grp", "row"), None),
        P(),
        P("grp", "row", None, None, None),
        P("grp", "row", None),
        P("grp", "row"),
        P(("grp", "row"), None),
    )
    return jax.shard_map(
        body,
        mesh=mesh,
        in_specs=placed,
        out_specs=(P(("grp", "row"), None), P(), P(("grp", "row"), None)),
        check_vma=False,
    )
```

```python
import functools
import math

import jax
import jax.numpy as jnp
from jax import lax
from jax.experimental import pallas as pl
from jax.experimental.pallas import tpu as pltpu
from jax.sharding import PartitionSpec as P

VMEM_LIMIT = 60 * 1024 * 1024


def silu_slope(pre):
    sigma = jax.nn.sigmoid(pre)
    return sigma * (1.0 + pre * (1.0 - sigma))


def aggregate_kernel(cols_ref, count_ref, vals_hbm, panel_hbm, out_ref, vals, panel, sems):
    row_blocks, slot_total, block, _ = vals.shape
    col_blocks = panel.shape[0] // block
    load_vals = pltpu.make_async_copy(vals_hbm, vals, sems.at[0])
    load_panel = pltpu.make_async_copy(panel_hbm, panel, sems.at[1])
    load_vals.start()
    load_panel.start()
    load_vals.wait()
    load_panel.wait()
    for t in range(row_blocks):
        live = jnp.clip(count_ref[t], 0, slot_total)

        def body(k, acc):
            col = jnp.clip(cols_ref[t, k], 0, col_blocks - 1)
            start = pl.multiple_of(col * block, block)
            return acc + jnp.dot(
                vals[t, k], panel[pl.ds(start, block), :], preferred_element_type=jnp.float32
            )

        out_ref[t] = lax.fori_loop(0, live, body, jnp.zeros(out_ref.shape[1:], jnp.float32))


def spread_kernel(side_ref, cols_ref, count_ref, vals_hbm, grad_ref, out_hbm, vals, total, sems):
    row_blocks, slot_total, block, _ = vals.shape
    per_panel = grad_ref.shape[1]
    col_blocks = total.shape[0]
    load_vals = pltpu.make_async_copy(vals_hbm, vals, sems.at[0])
    load_vals.start()

    def clear(c, carry):
        total[c] = jnp.zeros(total.shape[1:], total.dtype)
        return carry

    lax.fori_loop(0, col_blocks, clear, 0)
    load_vals.wait()
    for t in range(row_blocks):
        live = jnp.clip(count_ref[t], 0, slot_total)
        panel, within = divmod(t, per_panel)
        grad = grad_ref[jnp.where(side_ref[0] == panel, 0, 1), within]

        def body(k, carry):
            col = jnp.clip(cols_ref[t, k], 0, col_blocks - 1)
            contrib = lax.dot_general(
                vals[t, k], grad, (((0,), (0,)), ((), ())), preferred_element_type=jnp.float32
            )
            total[col] += contrib
            return carry

        lax.fori_loop(0, live, body, 0)
    store = pltpu.make_async_copy(total, out_hbm, sems.at[1])
    store.start()
    store.wait()


def aggregate(cols, count, vals, panel):
    row_blocks, slot_total, block, _ = vals.shape
    width = panel.shape[1]
    return pl.pallas_call(
        aggregate_kernel,
        out_shape=jax.ShapeDtypeStruct((row_blocks, block, width), jnp.float32),
        in_specs=[
            pl.BlockSpec(memory_space=pltpu.SMEM),
            pl.BlockSpec(memory_space=pltpu.SMEM),
            pl.BlockSpec(memory_space=pl.ANY),
            pl.BlockSpec(memory_space=pl.ANY),
        ],
        out_specs=pl.BlockSpec(memory_space=pltpu.VMEM),
        scratch_shapes=[
            pltpu.VMEM(vals.shape, vals.dtype),
            pltpu.VMEM(panel.shape, panel.dtype),
            pltpu.SemaphoreType.DMA((2,)),
        ],
        compiler_params=pltpu.CompilerParams(vmem_limit_bytes=VMEM_LIMIT),
        cost_estimate=pl.CostEstimate(
            flops=2 * row_blocks * slot_total * block * block * width,
            bytes_accessed=vals.size * 2 + panel.size * 2 + row_blocks * block * width * 4,
            transcendentals=0,
        ),
    )(cols, count, vals, panel)


def spread(side, cols, count, vals, grad, col_blocks):
    row_blocks, slot_total, block, _ = vals.shape
    width = grad.shape[-1]
    return pl.pallas_call(
        spread_kernel,
        out_shape=jax.ShapeDtypeStruct((col_blocks, block, width), jnp.float32),
        in_specs=[
            pl.BlockSpec(memory_space=pltpu.SMEM),
            pl.BlockSpec(memory_space=pltpu.SMEM),
            pl.BlockSpec(memory_space=pltpu.SMEM),
            pl.BlockSpec(memory_space=pl.ANY),
            pl.BlockSpec(memory_space=pltpu.VMEM),
        ],
        out_specs=pl.BlockSpec(memory_space=pl.ANY),
        scratch_shapes=[
            pltpu.VMEM(vals.shape, vals.dtype),
            pltpu.VMEM((col_blocks, block, width), jnp.float32),
            pltpu.SemaphoreType.DMA((2,)),
        ],
        compiler_params=pltpu.CompilerParams(vmem_limit_bytes=VMEM_LIMIT),
        cost_estimate=pl.CostEstimate(
            flops=2 * row_blocks * slot_total * block * block * width,
            bytes_accessed=vals.size * 2 + grad.size * 2 + col_blocks * block * width * 4,
            transcendentals=0,
        ),
    )(side, cols, count, vals, grad)


def swap(value, axis):
    size = lax.axis_size(axis)
    return lax.ppermute(value, axis, [(i, i ^ 1) for i in range(size)])


def all_sum(value, axis):
    size = lax.axis_size(axis)
    step = 1
    while step < size:
        value = value + lax.ppermute(value, axis, [(i, i ^ step) for i in range(size)])
        step *= 2
    return value


def body(features, weight, block_vals, block_cols, block_count, cotangent):
    rows_dev, width = features.shape
    block = block_vals.shape[-1]
    groups = lax.axis_size("grp")
    members = lax.axis_size("row")
    verts = rows_dev * groups * members
    side = lax.axis_index("grp")
    gathered = lax.all_gather(features, "row", axis=0, tiled=True)
    col_blocks = gathered.shape[0] // block
    cols = block_cols[0]
    count = block_count[0]
    vals = block_vals[0]

    partial_value = aggregate(cols, count, vals, gathered).reshape(-1, width)
    mine = lax.dynamic_slice_in_dim(partial_value, side * rows_dev, rows_dev)
    theirs = lax.dynamic_slice_in_dim(partial_value, (1 - side) * rows_dev, rows_dev)
    summed = mine + swap(theirs, "grp")
    aggregated = summed.astype(jnp.bfloat16)
    pre = jnp.dot(aggregated, weight, preferred_element_type=jnp.float32)
    activated = jax.nn.silu(pre).astype(jnp.bfloat16)
    pre_grad = (cotangent.astype(jnp.float32) * silu_slope(pre)).astype(jnp.bfloat16)
    local_grad = jnp.dot(aggregated.T, pre_grad, preferred_element_type=jnp.float32)
    own_grad = jnp.dot(pre_grad, weight.T, preferred_element_type=jnp.float32).astype(jnp.bfloat16)
    both_grad = jnp.stack([own_grad, swap(own_grad, "grp")]).reshape(2, -1, block, width)
    weight_grad = all_sum(all_sum(local_grad, "row"), "grp") * (1.0 / math.sqrt(verts))

    term = spread(side.reshape(1), cols, count, vals, both_grad, col_blocks).reshape(-1, width)
    input_grad = lax.psum_scatter(term, "row", scatter_dimension=0, tiled=True).astype(jnp.bfloat16)
    return (activated, weight_grad, input_grad)


def solution(mesh):
    placed = (
        P(("grp", "row"), None),
        P(),
        P("grp", "row", None, None, None),
        P("grp", "row", None),
        P("grp", "row"),
        P(("grp", "row"), None),
    )
    return jax.shard_map(
        body,
        mesh=mesh,
        in_specs=placed,
        out_specs=(P(("grp", "row"), None), P(), P(("grp", "row"), None)),
        check_vma=False,
    )
```

```python
import functools
import math

import jax
import jax.numpy as jnp
from jax import lax
from jax.experimental import pallas as pl
from jax.experimental.pallas import tpu as pltpu
from jax.sharding import PartitionSpec as P

VMEM_LIMIT = 60 * 1024 * 1024


def silu_slope(pre):
    sigma = jax.nn.sigmoid(pre)
    return sigma * (1.0 + pre * (1.0 - sigma))


def aggregate_kernel(cols_ref, count_ref, vals_hbm, panel_hbm, out_ref, vals, panel, sems):
    row_blocks, slot_total, block, _ = vals.shape
    col_blocks = panel.shape[0] // block
    load_vals = pltpu.make_async_copy(vals_hbm, vals, sems.at[0])
    load_panel = pltpu.make_async_copy(panel_hbm, panel, sems.at[1])
    load_vals.start()
    load_panel.start()
    load_vals.wait()
    load_panel.wait()
    for t in range(row_blocks):
        live = jnp.clip(count_ref[t], 0, slot_total)

        def body(k, acc):
            col = jnp.clip(cols_ref[t, k], 0, col_blocks - 1)
            start = pl.multiple_of(col * block, block)
            return acc + jnp.dot(
                vals[t, k], panel[pl.ds(start, block), :], preferred_element_type=jnp.float32
            )

        out_ref[t] = lax.fori_loop(0, live, body, jnp.zeros(out_ref.shape[1:], jnp.float32))


def owner_slot(col, me, per_dev):
    owner, q = col // per_dev, col % per_dev
    dk = (owner % 2) ^ (me % 2)
    dx = ((owner // 2) % 4 - (me // 2) % 4 + 4) % 4
    dy = ((owner // 8) % 2) ^ ((me // 8) % 2)
    dz = ((owner // 16) - (me // 16) + 4) % 4
    half, q2 = q // 2, q % 2
    first = jnp.where(half == 0, dx, dz)
    second = jnp.where(half == 0, dz, dx)
    return (dk * 2 + half) * 64 + ((first * 4 + second) * 2 + dy) * 2 + q2


def spread_kernel(side_ref, cols_ref, count_ref, vals_hbm, grad_ref, out_hbm, vals, total, sems):
    row_blocks, slot_total, block, _ = vals.shape
    per_panel = grad_ref.shape[1]
    col_blocks = total.shape[0]
    per_dev = col_blocks // 64
    me = side_ref[1]
    load_vals = pltpu.make_async_copy(vals_hbm, vals, sems.at[0])
    load_vals.start()

    def clear(c, carry):
        total[c] = jnp.zeros(total.shape[1:], total.dtype)
        return carry

    lax.fori_loop(0, col_blocks, clear, 0)
    load_vals.wait()
    for t in range(row_blocks):
        live = jnp.clip(count_ref[t], 0, slot_total)
        panel, within = divmod(t, per_panel)
        grad = grad_ref[jnp.where(side_ref[0] == panel, 0, 1), within]

        def body(k, carry):
            col = jnp.clip(cols_ref[t, k], 0, col_blocks - 1)
            contrib = lax.dot_general(
                vals[t, k], grad, (((0,), (0,)), ((), ())), preferred_element_type=jnp.float32
            )
            slot = owner_slot(col, me, per_dev)
            total[slot] += contrib
            return carry

        lax.fori_loop(0, live, body, 0)
    store = pltpu.make_async_copy(total, out_hbm, sems.at[1])
    store.start()
    store.wait()


def aggregate(cols, count, vals, panel):
    row_blocks, slot_total, block, _ = vals.shape
    width = panel.shape[1]
    return pl.pallas_call(
        aggregate_kernel,
        out_shape=jax.ShapeDtypeStruct((row_blocks, block, width), jnp.float32),
        in_specs=[
            pl.BlockSpec(memory_space=pltpu.SMEM),
            pl.BlockSpec(memory_space=pltpu.SMEM),
            pl.BlockSpec(memory_space=pl.ANY),
            pl.BlockSpec(memory_space=pl.ANY),
        ],
        out_specs=pl.BlockSpec(memory_space=pltpu.VMEM),
        scratch_shapes=[
            pltpu.VMEM(vals.shape, vals.dtype),
            pltpu.VMEM(panel.shape, panel.dtype),
            pltpu.SemaphoreType.DMA((2,)),
        ],
        compiler_params=pltpu.CompilerParams(vmem_limit_bytes=VMEM_LIMIT),
        cost_estimate=pl.CostEstimate(
            flops=2 * row_blocks * slot_total * block * block * width,
            bytes_accessed=vals.size * 2 + panel.size * 2 + row_blocks * block * width * 4,
            transcendentals=0,
        ),
    )(cols, count, vals, panel)


def spread(side, cols, count, vals, grad, col_blocks):
    row_blocks, slot_total, block, _ = vals.shape
    width = grad.shape[-1]
    return pl.pallas_call(
        spread_kernel,
        out_shape=jax.ShapeDtypeStruct((col_blocks, block, width), jnp.float32),
        in_specs=[
            pl.BlockSpec(memory_space=pltpu.SMEM),
            pl.BlockSpec(memory_space=pltpu.SMEM),
            pl.BlockSpec(memory_space=pltpu.SMEM),
            pl.BlockSpec(memory_space=pl.ANY),
            pl.BlockSpec(memory_space=pltpu.VMEM),
        ],
        out_specs=pl.BlockSpec(memory_space=pl.ANY),
        scratch_shapes=[
            pltpu.VMEM(vals.shape, vals.dtype),
            pltpu.VMEM((col_blocks, block, width), jnp.float32),
            pltpu.SemaphoreType.DMA((2,)),
        ],
        compiler_params=pltpu.CompilerParams(vmem_limit_bytes=VMEM_LIMIT),
        cost_estimate=pl.CostEstimate(
            flops=2 * row_blocks * slot_total * block * block * width,
            bytes_accessed=vals.size * 2 + grad.size * 2 + col_blocks * block * width * 4,
            transcendentals=0,
        ),
    )(side, cols, count, vals, grad)


def swap(value, axis):
    size = lax.axis_size(axis)
    return lax.ppermute(value, axis, [(i, i ^ 1) for i in range(size)])


def shifted(value, digit, size, shift):
    def dest(r):
        place = (r // digit) % size
        return r + (((place + shift) % size) - place) * digit

    return lax.ppermute(value, "row", [(r, dest(r)) for r in range(64)])


def row_reduce_scatter(term):
    _, block, width = term.shape
    staged = term.reshape(2, 2, 64, block, width)
    level = staged[0] + shifted(staged[1], 1, 2, 1)
    first = level[0].reshape(4, 16, block, width)
    second = level[1].reshape(4, 16, block, width)
    first = first[0] + sum(shifted(first[s], 2, 4, s) for s in range(1, 4))
    second = second[0] + sum(shifted(second[s], 16, 4, s) for s in range(1, 4))
    first = first.reshape(4, 4, block, width)
    second = second.reshape(4, 4, block, width)
    first = first[0] + sum(shifted(first[s], 16, 4, s) for s in range(1, 4))
    second = second[0] + sum(shifted(second[s], 2, 4, s) for s in range(1, 4))
    first = first.reshape(2, 2, block, width)
    second = second.reshape(2, 2, block, width)
    first = first[0] + shifted(first[1], 8, 2, 1)
    second = second[0] + shifted(second[1], 8, 2, 1)
    return jnp.concatenate([first, second]).reshape(-1, width)


def all_sum(value, axis):
    size = lax.axis_size(axis)
    step = 1
    while step < size:
        value = value + lax.ppermute(value, axis, [(i, i ^ step) for i in range(size)])
        step *= 2
    return value


def body(features, weight, block_vals, block_cols, block_count, cotangent):
    rows_dev, width = features.shape
    block = block_vals.shape[-1]
    groups = lax.axis_size("grp")
    members = lax.axis_size("row")
    verts = rows_dev * groups * members
    side = lax.axis_index("grp")
    gathered = lax.all_gather(features, "row", axis=0, tiled=True)
    col_blocks = gathered.shape[0] // block
    cols = block_cols[0]
    count = block_count[0]
    vals = block_vals[0]

    partial_value = aggregate(cols, count, vals, gathered).reshape(-1, width)
    mine = lax.dynamic_slice_in_dim(partial_value, side * rows_dev, rows_dev)
    theirs = lax.dynamic_slice_in_dim(partial_value, (1 - side) * rows_dev, rows_dev)
    summed = mine + swap(theirs, "grp")
    aggregated = summed.astype(jnp.bfloat16)
    pre = jnp.dot(aggregated, weight, preferred_element_type=jnp.float32)
    activated = jax.nn.silu(pre).astype(jnp.bfloat16)
    pre_grad = (cotangent.astype(jnp.float32) * silu_slope(pre)).astype(jnp.bfloat16)
    local_grad = jnp.dot(aggregated.T, pre_grad, preferred_element_type=jnp.float32)
    own_grad = jnp.dot(pre_grad, weight.T, preferred_element_type=jnp.float32).astype(jnp.bfloat16)
    both_grad = jnp.stack([own_grad, swap(own_grad, "grp")]).reshape(2, -1, block, width)
    weight_grad = all_sum(all_sum(local_grad, "row"), "grp") * (1.0 / math.sqrt(verts))

    where = jnp.stack([side, lax.axis_index("row")]).astype(jnp.int32)
    term = spread(where, cols, count, vals, both_grad, col_blocks)
    input_grad = row_reduce_scatter(term).astype(jnp.bfloat16)
    return (activated, weight_grad, input_grad)


def solution(mesh):
    placed = (
        P(("grp", "row"), None),
        P(),
        P("grp", "row", None, None, None),
        P("grp", "row", None),
        P("grp", "row"),
        P(("grp", "row"), None),
    )
    return jax.shard_map(
        body,
        mesh=mesh,
        in_specs=placed,
        out_specs=(P(("grp", "row"), None), P(), P(("grp", "row"), None)),
        check_vma=False,
    )
```

```python
import functools
import math

import jax
import jax.numpy as jnp
from jax import lax
from jax.experimental import pallas as pl
from jax.experimental.pallas import tpu as pltpu
from jax.sharding import PartitionSpec as P

VMEM_LIMIT = 60 * 1024 * 1024


def silu_slope(pre):
    sigma = jax.nn.sigmoid(pre)
    return sigma * (1.0 + pre * (1.0 - sigma))


def aggregate_kernel(cols_ref, count_ref, vals_hbm, panel_hbm, out_ref, vals, panel, sems):
    row_blocks, slot_total, block, _ = vals.shape
    col_blocks = panel.shape[0] // block
    load_vals = pltpu.make_async_copy(vals_hbm, vals, sems.at[0])
    load_panel = pltpu.make_async_copy(panel_hbm, panel, sems.at[1])
    load_vals.start()
    load_panel.start()
    load_vals.wait()
    load_panel.wait()
    for t in range(row_blocks):
        live = jnp.clip(count_ref[t], 0, slot_total)

        def body(k, acc):
            col = jnp.clip(cols_ref[t, k], 0, col_blocks - 1)
            start = pl.multiple_of(col * block, block)
            return acc + jnp.dot(
                vals[t, k], panel[pl.ds(start, block), :], preferred_element_type=jnp.float32
            )

        out_ref[t] = lax.fori_loop(0, live, body, jnp.zeros(out_ref.shape[1:], jnp.float32))


def owner_slot(col, me, per_dev):
    owner, q = col // per_dev, col % per_dev
    dk = (owner % 2) ^ (me % 2)
    dx = ((owner // 2) % 4 - (me // 2) % 4 + 4) % 4
    dy = ((owner // 8) % 2) ^ ((me // 8) % 2)
    dz = ((owner // 16) - (me // 16) + 4) % 4
    half, q2 = q // 2, q % 2
    first = jnp.where(half == 0, dx, dz)
    second = jnp.where(half == 0, dz, dx)
    return (dk * 2 + half) * 64 + ((first * 4 + second) * 2 + dy) * 2 + q2


def spread_kernel(side_ref, cols_ref, count_ref, vals_hbm, grad_ref, keep_hbm, send_hbm, vals, total, sems):
    row_blocks, slot_total, block, _ = vals.shape
    per_panel = grad_ref.shape[1]
    col_blocks = total.shape[0]
    per_dev = col_blocks // 64
    me = side_ref[1]
    load_vals = pltpu.make_async_copy(vals_hbm, vals, sems.at[0])
    load_vals.start()

    def clear(c, carry):
        total[c] = jnp.zeros(total.shape[1:], total.dtype)
        return carry

    lax.fori_loop(0, col_blocks, clear, 0)
    load_vals.wait()
    for t in range(row_blocks):
        live = jnp.clip(count_ref[t], 0, slot_total)
        panel, within = divmod(t, per_panel)
        grad = grad_ref[jnp.where(side_ref[0] == panel, 0, 1), within]

        def body(k, carry):
            col = jnp.clip(cols_ref[t, k], 0, col_blocks - 1)
            contrib = lax.dot_general(
                vals[t, k], grad, (((0,), (0,)), ((), ())), preferred_element_type=jnp.float32
            )
            slot = owner_slot(col, me, per_dev)
            total[slot] += contrib
            return carry

        lax.fori_loop(0, live, body, 0)
    half = col_blocks // 2
    keep = pltpu.make_async_copy(total.at[pl.ds(0, half)], keep_hbm, sems.at[1])
    send = pltpu.make_async_copy(total.at[pl.ds(half, half)], send_hbm, sems.at[2])
    send.start()
    keep.start()
    send.wait()
    keep.wait()


def aggregate(cols, count, vals, panel):
    row_blocks, slot_total, block, _ = vals.shape
    width = panel.shape[1]
    return pl.pallas_call(
        aggregate_kernel,
        out_shape=jax.ShapeDtypeStruct((row_blocks, block, width), jnp.float32),
        in_specs=[
            pl.BlockSpec(memory_space=pltpu.SMEM),
            pl.BlockSpec(memory_space=pltpu.SMEM),
            pl.BlockSpec(memory_space=pl.ANY),
            pl.BlockSpec(memory_space=pl.ANY),
        ],
        out_specs=pl.BlockSpec(memory_space=pltpu.VMEM),
        scratch_shapes=[
            pltpu.VMEM(vals.shape, vals.dtype),
            pltpu.VMEM(panel.shape, panel.dtype),
            pltpu.SemaphoreType.DMA((2,)),
        ],
        compiler_params=pltpu.CompilerParams(vmem_limit_bytes=VMEM_LIMIT),
        cost_estimate=pl.CostEstimate(
            flops=2 * row_blocks * slot_total * block * block * width,
            bytes_accessed=vals.size * 2 + panel.size * 2 + row_blocks * block * width * 4,
            transcendentals=0,
        ),
    )(cols, count, vals, panel)


def spread(side, cols, count, vals, grad, col_blocks):
    row_blocks, slot_total, block, _ = vals.shape
    width = grad.shape[-1]
    return pl.pallas_call(
        spread_kernel,
        out_shape=[jax.ShapeDtypeStruct((col_blocks // 2, block, width), jnp.float32)] * 2,
        in_specs=[
            pl.BlockSpec(memory_space=pltpu.SMEM),
            pl.BlockSpec(memory_space=pltpu.SMEM),
            pl.BlockSpec(memory_space=pltpu.SMEM),
            pl.BlockSpec(memory_space=pl.ANY),
            pl.BlockSpec(memory_space=pltpu.VMEM),
        ],
        out_specs=[pl.BlockSpec(memory_space=pl.ANY)] * 2,
        scratch_shapes=[
            pltpu.VMEM(vals.shape, vals.dtype),
            pltpu.VMEM((col_blocks, block, width), jnp.float32),
            pltpu.SemaphoreType.DMA((3,)),
        ],
        compiler_params=pltpu.CompilerParams(vmem_limit_bytes=VMEM_LIMIT),
        cost_estimate=pl.CostEstimate(
            flops=2 * row_blocks * slot_total * block * block * width,
            bytes_accessed=vals.size * 2 + grad.size * 2 + col_blocks * block * width * 4,
            transcendentals=0,
        ),
    )(side, cols, count, vals, grad)


def swap(value, axis):
    size = lax.axis_size(axis)
    return lax.ppermute(value, axis, [(i, i ^ 1) for i in range(size)])


def shifted(value, digit, size, shift):
    def dest(r):
        place = (r // digit) % size
        return r + (((place + shift) % size) - place) * digit

    return lax.ppermute(value, "row", [(r, dest(r)) for r in range(64)])


def row_reduce_scatter(keep, send):
    _, block, width = keep.shape
    keep = keep.reshape(2, 4, 16, block, width)
    came = shifted(send, 1, 2, 1).reshape(2, 4, 16, block, width)
    first = [keep[0, s] + came[0, s] for s in range(4)]
    second = [keep[1, s] + came[1, s] for s in range(4)]
    first = (first[0] + sum(shifted(first[s], 2, 4, s) for s in range(1, 4))).reshape(4, 4, block, width)
    second = (second[0] + sum(shifted(second[s], 16, 4, s) for s in range(1, 4))).reshape(4, 4, block, width)
    first = (first[0] + sum(shifted(first[s], 16, 4, s) for s in range(1, 4))).reshape(2, 2, block, width)
    second = (second[0] + sum(shifted(second[s], 2, 4, s) for s in range(1, 4))).reshape(2, 2, block, width)
    first = first[0] + shifted(first[1], 8, 2, 1)
    second = second[0] + shifted(second[1], 8, 2, 1)
    return jnp.concatenate([first, second]).reshape(-1, width)


def all_sum(value, axis):
    size = lax.axis_size(axis)
    step = 1
    while step < size:
        value = value + lax.ppermute(value, axis, [(i, i ^ step) for i in range(size)])
        step *= 2
    return value


def body(features, weight, block_vals, block_cols, block_count, cotangent):
    rows_dev, width = features.shape
    block = block_vals.shape[-1]
    groups = lax.axis_size("grp")
    members = lax.axis_size("row")
    verts = rows_dev * groups * members
    side = lax.axis_index("grp")
    gathered = lax.all_gather(features, "row", axis=0, tiled=True)
    col_blocks = gathered.shape[0] // block
    cols = block_cols[0]
    count = block_count[0]
    vals = block_vals[0]

    partial_value = aggregate(cols, count, vals, gathered).reshape(-1, width)
    mine = lax.dynamic_slice_in_dim(partial_value, side * rows_dev, rows_dev)
    theirs = lax.dynamic_slice_in_dim(partial_value, (1 - side) * rows_dev, rows_dev)
    summed = mine + swap(theirs, "grp")
    aggregated = summed.astype(jnp.bfloat16)
    pre = jnp.dot(aggregated, weight, preferred_element_type=jnp.float32)
    activated = jax.nn.silu(pre).astype(jnp.bfloat16)
    pre_grad = (cotangent.astype(jnp.float32) * silu_slope(pre)).astype(jnp.bfloat16)
    local_grad = jnp.dot(aggregated.T, pre_grad, preferred_element_type=jnp.float32)
    own_grad = jnp.dot(pre_grad, weight.T, preferred_element_type=jnp.float32).astype(jnp.bfloat16)
    both_grad = jnp.stack([own_grad, swap(own_grad, "grp")]).reshape(2, -1, block, width)
    weight_grad = lax.psum(local_grad, ("grp", "row")) * (1.0 / math.sqrt(verts))

    where = jnp.stack([side, lax.axis_index("row")]).astype(jnp.int32)
    keep, send = spread(where, cols, count, vals, both_grad, col_blocks)
    input_grad = row_reduce_scatter(keep, send).astype(jnp.bfloat16)
    return (activated, weight_grad, input_grad)


def solution(mesh):
    placed = (
        P(("grp", "row"), None),
        P(),
        P("grp", "row", None, None, None),
        P("grp", "row", None),
        P("grp", "row"),
        P(("grp", "row"), None),
    )
    return jax.shard_map(
        body,
        mesh=mesh,
        in_specs=placed,
        out_specs=(P(("grp", "row"), None), P(), P(("grp", "row"), None)),
        check_vma=False,
    )
```

```python
import functools
import math

import jax
import jax.numpy as jnp
from jax import lax
from jax.experimental import pallas as pl
from jax.experimental.pallas import tpu as pltpu
from jax.sharding import PartitionSpec as P

VMEM_LIMIT = 60 * 1024 * 1024


def silu_slope(pre):
    sigma = jax.nn.sigmoid(pre)
    return sigma * (1.0 + pre * (1.0 - sigma))


def aggregate_kernel(cols_ref, count_ref, vals_hbm, panel_hbm, out_ref, vals, panel, sems):
    row_blocks, slot_total, block, _ = vals.shape
    col_blocks = panel.shape[0] // block
    load_vals = pltpu.make_async_copy(vals_hbm, vals, sems.at[0])
    load_panel = pltpu.make_async_copy(panel_hbm, panel, sems.at[1])
    load_vals.start()
    load_panel.start()
    load_vals.wait()
    load_panel.wait()
    for t in range(row_blocks):
        live = jnp.clip(count_ref[t], 0, slot_total)

        def body(k, acc):
            col = jnp.clip(cols_ref[t, k], 0, col_blocks - 1)
            start = pl.multiple_of(col * block, block)
            return acc + jnp.dot(
                vals[t, k], panel[pl.ds(start, block), :], preferred_element_type=jnp.float32
            )

        out_ref[t] = lax.fori_loop(0, live, body, jnp.zeros(out_ref.shape[1:], jnp.float32))


def owner_slot(col, me, per_dev):
    owner, q = col // per_dev, col % per_dev
    dk = (owner % 2) ^ (me % 2)
    dx = ((owner // 2) % 4 - (me // 2) % 4 + 4) % 4
    dy = ((owner // 8) % 2) ^ ((me // 8) % 2)
    dz = ((owner // 16) - (me // 16) + 4) % 4
    half, q2 = q // 2, q % 2
    first = jnp.where(half == 0, dx, dz)
    second = jnp.where(half == 0, dz, dx)
    return (dk * 2 + half) * 64 + ((first * 4 + second) * 2 + dy) * 2 + q2


def spread_kernel(side_ref, cols_ref, count_ref, vals_hbm, grad_ref, keep_hbm, send_hbm, vals, total, sems):
    row_blocks, slot_total, block, _ = vals.shape
    per_panel = grad_ref.shape[1]
    col_blocks = total.shape[0]
    per_dev = col_blocks // 64
    me = side_ref[1]
    load_vals = pltpu.make_async_copy(vals_hbm, vals, sems.at[0])
    load_vals.start()

    def clear(c, carry):
        total[c] = jnp.zeros(total.shape[1:], total.dtype)
        return carry

    lax.fori_loop(0, col_blocks, clear, 0)
    load_vals.wait()
    for t in range(row_blocks):
        live = jnp.clip(count_ref[t], 0, slot_total)
        panel, within = divmod(t, per_panel)
        grad = grad_ref[jnp.where(side_ref[0] == panel, 0, 1), within]

        def body(k, carry):
            col = jnp.clip(cols_ref[t, k], 0, col_blocks - 1)
            contrib = lax.dot_general(
                vals[t, k], grad, (((0,), (0,)), ((), ())), preferred_element_type=jnp.float32
            )
            slot = owner_slot(col, me, per_dev)
            total[slot] += contrib
            return carry

        lax.fori_loop(0, live, body, 0)
    half = col_blocks // 2
    keep = pltpu.make_async_copy(total.at[pl.ds(0, half)], keep_hbm, sems.at[1])
    send = pltpu.make_async_copy(total.at[pl.ds(half, half)], send_hbm, sems.at[2])
    send.start()
    keep.start()
    send.wait()
    keep.wait()


def aggregate(cols, count, vals, panel):
    row_blocks, slot_total, block, _ = vals.shape
    width = panel.shape[1]
    return pl.pallas_call(
        aggregate_kernel,
        out_shape=jax.ShapeDtypeStruct((row_blocks, block, width), jnp.float32),
        in_specs=[
            pl.BlockSpec(memory_space=pltpu.SMEM),
            pl.BlockSpec(memory_space=pltpu.SMEM),
            pl.BlockSpec(memory_space=pl.ANY),
            pl.BlockSpec(memory_space=pl.ANY),
        ],
        out_specs=pl.BlockSpec(memory_space=pltpu.VMEM),
        scratch_shapes=[
            pltpu.VMEM(vals.shape, vals.dtype),
            pltpu.VMEM(panel.shape, panel.dtype),
            pltpu.SemaphoreType.DMA((2,)),
        ],
        compiler_params=pltpu.CompilerParams(vmem_limit_bytes=VMEM_LIMIT),
        cost_estimate=pl.CostEstimate(
            flops=2 * row_blocks * slot_total * block * block * width,
            bytes_accessed=vals.size * 2 + panel.size * 2 + row_blocks * block * width * 4,
            transcendentals=0,
        ),
    )(cols, count, vals, panel)


def spread(side, cols, count, vals, grad, col_blocks):
    row_blocks, slot_total, block, _ = vals.shape
    width = grad.shape[-1]
    return pl.pallas_call(
        spread_kernel,
        out_shape=[jax.ShapeDtypeStruct((col_blocks // 2, block, width), jnp.float32)] * 2,
        in_specs=[
            pl.BlockSpec(memory_space=pltpu.SMEM),
            pl.BlockSpec(memory_space=pltpu.SMEM),
            pl.BlockSpec(memory_space=pltpu.SMEM),
            pl.BlockSpec(memory_space=pl.ANY),
            pl.BlockSpec(memory_space=pltpu.VMEM),
        ],
        out_specs=[pl.BlockSpec(memory_space=pl.ANY)] * 2,
        scratch_shapes=[
            pltpu.VMEM(vals.shape, vals.dtype),
            pltpu.VMEM((col_blocks, block, width), jnp.float32),
            pltpu.SemaphoreType.DMA((3,)),
        ],
        compiler_params=pltpu.CompilerParams(vmem_limit_bytes=VMEM_LIMIT),
        cost_estimate=pl.CostEstimate(
            flops=2 * row_blocks * slot_total * block * block * width,
            bytes_accessed=vals.size * 2 + grad.size * 2 + col_blocks * block * width * 4,
            transcendentals=0,
        ),
    )(side, cols, count, vals, grad)


def swap(value, axis):
    size = lax.axis_size(axis)
    return lax.ppermute(value, axis, [(i, i ^ 1) for i in range(size)])


def shifted(value, digit, size, shift):
    def dest(r):
        place = (r // digit) % size
        return r + (((place + shift) % size) - place) * digit

    return lax.ppermute(value, "row", [(r, dest(r)) for r in range(64)])


def row_reduce_scatter(keep, send):
    _, block, width = keep.shape
    keep = keep.reshape(2, 4, 16, block, width)
    came = shifted(send, 1, 2, 1).reshape(2, 4, 16, block, width)
    first = [keep[0, s] + came[0, s] for s in range(4)]
    second = [keep[1, s] + came[1, s] for s in range(4)]
    first = (first[0] + sum(shifted(first[s], 2, 4, s) for s in range(1, 4))).reshape(4, 4, block, width)
    second = (second[0] + sum(shifted(second[s], 16, 4, s) for s in range(1, 4))).reshape(4, 4, block, width)
    first = (first[0] + sum(shifted(first[s], 16, 4, s) for s in range(1, 4))).reshape(2, 2, block, width)
    second = (second[0] + sum(shifted(second[s], 2, 4, s) for s in range(1, 4))).reshape(2, 2, block, width)
    first = first[0] + shifted(first[1], 8, 2, 1)
    second = second[0] + shifted(second[1], 8, 2, 1)
    return jnp.concatenate([first, second]).reshape(-1, width)


def all_sum(value, axis):
    size = lax.axis_size(axis)
    step = 1
    while step < size:
        value = value + lax.ppermute(value, axis, [(i, i ^ step) for i in range(size)])
        step *= 2
    return value


def body(features, weight, block_vals, block_cols, block_count, cotangent):
    rows_dev, width = features.shape
    block = block_vals.shape[-1]
    groups = lax.axis_size("grp")
    members = lax.axis_size("row")
    verts = rows_dev * groups * members
    side = lax.axis_index("grp")
    gathered = lax.all_gather(features, "row", axis=0, tiled=True)
    col_blocks = gathered.shape[0] // block
    cols = block_cols[0]
    count = block_count[0]
    vals = block_vals[0]

    partial_value = aggregate(cols, count, vals, gathered).reshape(-1, width)
    mine = lax.dynamic_slice_in_dim(partial_value, side * rows_dev, rows_dev)
    theirs = lax.dynamic_slice_in_dim(partial_value, (1 - side) * rows_dev, rows_dev)
    summed = mine + swap(theirs, "grp")
    aggregated = summed.astype(jnp.bfloat16)
    pre = jnp.dot(aggregated, weight, preferred_element_type=jnp.float32)
    activated = jax.nn.silu(pre).astype(jnp.bfloat16)
    pre_grad = (cotangent.astype(jnp.float32) * silu_slope(pre)).astype(jnp.bfloat16)
    local_grad = jnp.dot(aggregated.T, pre_grad, preferred_element_type=jnp.float32)
    own_grad = jnp.dot(pre_grad, weight.T, preferred_element_type=jnp.float32).astype(jnp.bfloat16)
    both_grad = jnp.stack([own_grad, swap(own_grad, "grp")]).reshape(2, -1, block, width)
    weight_grad = all_sum(all_sum(local_grad, "grp"), "row")
    weight_grad, both_grad = lax.optimization_barrier((weight_grad, both_grad))
    weight_grad = weight_grad * (1.0 / math.sqrt(verts))

    where = jnp.stack([side, lax.axis_index("row")]).astype(jnp.int32)
    keep, send = spread(where, cols, count, vals, both_grad, col_blocks)
    input_grad = row_reduce_scatter(keep, send).astype(jnp.bfloat16)
    return (activated, weight_grad, input_grad)


def solution(mesh):
    placed = (
        P(("grp", "row"), None),
        P(),
        P("grp", "row", None, None, None),
        P("grp", "row", None),
        P("grp", "row"),
        P(("grp", "row"), None),
    )
    return jax.shard_map(
        body,
        mesh=mesh,
        in_specs=placed,
        out_specs=(P(("grp", "row"), None), P(), P(("grp", "row"), None)),
        check_vma=False,
    )
```

```python
import functools
import math

import jax
import jax.numpy as jnp
from jax import lax
from jax.experimental import pallas as pl
from jax.experimental.pallas import tpu as pltpu
from jax.sharding import PartitionSpec as P

VMEM_LIMIT = 60 * 1024 * 1024


def silu_slope(pre):
    sigma = jax.nn.sigmoid(pre)
    return sigma * (1.0 + pre * (1.0 - sigma))


def aggregate_kernel(cols_ref, count_ref, vals_hbm, panel_hbm, out_ref, vals, panel, sems):
    row_blocks, slot_total, block, _ = vals.shape
    col_blocks = panel.shape[0] // block
    load_vals = pltpu.make_async_copy(vals_hbm, vals, sems.at[0])
    load_panel = pltpu.make_async_copy(panel_hbm, panel, sems.at[1])
    load_vals.start()
    load_panel.start()
    load_vals.wait()
    load_panel.wait()
    for t in range(row_blocks):
        live = jnp.clip(count_ref[t], 0, slot_total)

        def body(k, acc):
            col = jnp.clip(cols_ref[t, k], 0, col_blocks - 1)
            start = pl.multiple_of(col * block, block)
            return acc + jnp.dot(
                vals[t, k], panel[pl.ds(start, block), :], preferred_element_type=jnp.float32
            )

        out_ref[t] = lax.fori_loop(0, live, body, jnp.zeros(out_ref.shape[1:], jnp.float32))


def owner_slot(col, me, per_dev):
    owner, q = col // per_dev, col % per_dev
    dk = (owner % 2) ^ (me % 2)
    dx = ((owner // 2) % 4 - (me // 2) % 4 + 4) % 4
    dy = ((owner // 8) % 2) ^ ((me // 8) % 2)
    dz = ((owner // 16) - (me // 16) + 4) % 4
    half, q2 = q // 2, q % 2
    first = jnp.where(half == 0, dx, dz)
    second = jnp.where(half == 0, dz, dx)
    return (dk * 2 + half) * 64 + ((first * 4 + second) * 2 + dy) * 2 + q2


def spread_kernel(side_ref, cols_ref, count_ref, vals_hbm, grad_ref, extra_ref, keep_hbm, send_hbm, vals, total, sems):
    row_blocks, slot_total, block, _ = vals.shape
    per_panel = grad_ref.shape[1]
    col_blocks = total.shape[0]
    per_dev = col_blocks // 64
    me = side_ref[1]
    load_vals = pltpu.make_async_copy(vals_hbm, vals, sems.at[0])
    load_vals.start()

    def clear(c, carry):
        total[c] = jnp.zeros(total.shape[1:], total.dtype)
        return carry

    lax.fori_loop(0, col_blocks, clear, 0)
    load_vals.wait()
    for t in range(row_blocks):
        live = jnp.clip(count_ref[t], 0, slot_total)
        panel, within = divmod(t, per_panel)
        grad = grad_ref[jnp.where(side_ref[0] == panel, 0, 1), within]

        def body(k, carry):
            col = jnp.clip(cols_ref[t, k], 0, col_blocks - 1)
            contrib = lax.dot_general(
                vals[t, k], grad, (((0,), (0,)), ((), ())), preferred_element_type=jnp.float32
            )
            slot = owner_slot(col, me, per_dev)
            total[slot] += contrib
            return carry

        lax.fori_loop(0, live, body, 0)
    half = col_blocks // 2
    keep = pltpu.make_async_copy(total.at[pl.ds(0, half)], keep_hbm, sems.at[1])
    send = pltpu.make_async_copy(total.at[pl.ds(half, half)], send_hbm.at[pl.ds(0, half)], sems.at[2])
    tail = pltpu.make_async_copy(extra_ref, send_hbm.at[pl.ds(half, extra_ref.shape[0])], sems.at[3])
    send.start()
    keep.start()
    tail.start()
    send.wait()
    keep.wait()
    tail.wait()


def aggregate(cols, count, vals, panel):
    row_blocks, slot_total, block, _ = vals.shape
    width = panel.shape[1]
    return pl.pallas_call(
        aggregate_kernel,
        out_shape=jax.ShapeDtypeStruct((row_blocks, block, width), jnp.float32),
        in_specs=[
            pl.BlockSpec(memory_space=pltpu.SMEM),
            pl.BlockSpec(memory_space=pltpu.SMEM),
            pl.BlockSpec(memory_space=pl.ANY),
            pl.BlockSpec(memory_space=pl.ANY),
        ],
        out_specs=pl.BlockSpec(memory_space=pltpu.VMEM),
        scratch_shapes=[
            pltpu.VMEM(vals.shape, vals.dtype),
            pltpu.VMEM(panel.shape, panel.dtype),
            pltpu.SemaphoreType.DMA((2,)),
        ],
        compiler_params=pltpu.CompilerParams(vmem_limit_bytes=VMEM_LIMIT),
        cost_estimate=pl.CostEstimate(
            flops=2 * row_blocks * slot_total * block * block * width,
            bytes_accessed=vals.size * 2 + panel.size * 2 + row_blocks * block * width * 4,
            transcendentals=0,
        ),
    )(cols, count, vals, panel)


def spread(side, cols, count, vals, grad, extra, col_blocks):
    row_blocks, slot_total, block, _ = vals.shape
    width = grad.shape[-1]
    return pl.pallas_call(
        spread_kernel,
        out_shape=[
            jax.ShapeDtypeStruct((col_blocks // 2, block, width), jnp.float32),
            jax.ShapeDtypeStruct((col_blocks // 2 + extra.shape[0], block, width), jnp.float32),
        ],
        in_specs=[
            pl.BlockSpec(memory_space=pltpu.SMEM),
            pl.BlockSpec(memory_space=pltpu.SMEM),
            pl.BlockSpec(memory_space=pltpu.SMEM),
            pl.BlockSpec(memory_space=pl.ANY),
            pl.BlockSpec(memory_space=pltpu.VMEM),
            pl.BlockSpec(memory_space=pltpu.VMEM),
        ],
        out_specs=[pl.BlockSpec(memory_space=pl.ANY)] * 2,
        scratch_shapes=[
            pltpu.VMEM(vals.shape, vals.dtype),
            pltpu.VMEM((col_blocks, block, width), jnp.float32),
            pltpu.SemaphoreType.DMA((4,)),
        ],
        compiler_params=pltpu.CompilerParams(vmem_limit_bytes=VMEM_LIMIT),
        cost_estimate=pl.CostEstimate(
            flops=2 * row_blocks * slot_total * block * block * width,
            bytes_accessed=vals.size * 2 + grad.size * 2 + col_blocks * block * width * 4,
            transcendentals=0,
        ),
    )(side, cols, count, vals, grad, extra)


def swap(value, axis):
    size = lax.axis_size(axis)
    return lax.ppermute(value, axis, [(i, i ^ 1) for i in range(size)])


def shifted(value, digit, size, shift):
    def dest(r):
        place = (r // digit) % size
        return r + (((place + shift) % size) - place) * digit

    return lax.ppermute(value, "row", [(r, dest(r)) for r in range(64)])


def ordered_sum(own, came, place, size):
    values = [own, *came]
    ordered = []
    for position in range(size):
        shift = (place - position + size) % size
        picked = values[0]
        for s in range(1, size):
            picked = jnp.where(shift == s, values[s], picked)
        ordered.append(picked)
    return (ordered[0] + ordered[1]) + (ordered[2] + ordered[3])


def row_reduce_scatter(keep, send, me):
    half, block, width = keep.shape
    extra = send.shape[0] - half
    keep = keep.reshape(2, 4, 16, block, width)
    came = shifted(send, 1, 2, 1)
    held = send[half:] + came[half:]
    came = came[:half].reshape(2, 4, 16, block, width)
    first = [keep[0, s] + came[0, s] for s in range(4)]
    second = [keep[1, s] + came[1, s] for s in range(4)]

    sent = [shifted(jnp.concatenate([first[s], held]), 2, 4, s) for s in range(1, 4)]
    held = ordered_sum(held, [m[16:] for m in sent], (me // 2) % 4, 4)
    first = (first[0] + sum(m[:16] for m in sent)).reshape(4, 4, block, width)
    second = (second[0] + sum(shifted(second[s], 16, 4, s) for s in range(1, 4))).reshape(4, 4, block, width)

    sent = [shifted(jnp.concatenate([first[s], held]), 16, 4, s) for s in range(1, 4)]
    held = ordered_sum(held, [m[4:] for m in sent], me // 16, 4)
    first = (first[0] + sum(m[:4] for m in sent)).reshape(2, 2, block, width)
    second = (second[0] + sum(shifted(second[s], 2, 4, s) for s in range(1, 4))).reshape(2, 2, block, width)

    sent = shifted(jnp.concatenate([first[1], held]), 8, 2, 1)
    held = held + sent[2:]
    first = first[0] + sent[:2]
    second = second[0] + shifted(second[1], 8, 2, 1)
    return jnp.concatenate([first, second]).reshape(-1, width), held


def all_sum(value, axis):
    size = lax.axis_size(axis)
    step = 1
    while step < size:
        value = value + lax.ppermute(value, axis, [(i, i ^ step) for i in range(size)])
        step *= 2
    return value


def body(features, weight, block_vals, block_cols, block_count, cotangent):
    rows_dev, width = features.shape
    block = block_vals.shape[-1]
    groups = lax.axis_size("grp")
    members = lax.axis_size("row")
    verts = rows_dev * groups * members
    side = lax.axis_index("grp")
    gathered = lax.all_gather(features, "row", axis=0, tiled=True)
    col_blocks = gathered.shape[0] // block
    cols = block_cols[0]
    count = block_count[0]
    vals = block_vals[0]

    partial_value = aggregate(cols, count, vals, gathered).reshape(-1, width)
    mine = lax.dynamic_slice_in_dim(partial_value, side * rows_dev, rows_dev)
    theirs = lax.dynamic_slice_in_dim(partial_value, (1 - side) * rows_dev, rows_dev)
    summed = mine + swap(theirs, "grp")
    aggregated = summed.astype(jnp.bfloat16)
    pre = jnp.dot(aggregated, weight, preferred_element_type=jnp.float32)
    activated = jax.nn.silu(pre).astype(jnp.bfloat16)
    pre_grad = (cotangent.astype(jnp.float32) * silu_slope(pre)).astype(jnp.bfloat16)
    local_grad = jnp.dot(aggregated.T, pre_grad, preferred_element_type=jnp.float32)
    own_grad = jnp.dot(pre_grad, weight.T, preferred_element_type=jnp.float32).astype(jnp.bfloat16)
    both_grad = jnp.stack([own_grad, swap(own_grad, "grp")]).reshape(2, -1, block, width)

    where = jnp.stack([side, lax.axis_index("row")]).astype(jnp.int32)
    extra = local_grad.reshape(-1, block, width)
    keep, send = spread(where, cols, count, vals, both_grad, extra, col_blocks)
    input_grad, held = row_reduce_scatter(keep, send, lax.axis_index("row"))
    input_grad = input_grad.astype(jnp.bfloat16)
    held = held.reshape(-1, width)
    weight_grad = (held + swap(held, "grp")) * (1.0 / math.sqrt(verts))
    return (activated, weight_grad, input_grad)


def solution(mesh):
    placed = (
        P(("grp", "row"), None),
        P(),
        P("grp", "row", None, None, None),
        P("grp", "row", None),
        P("grp", "row"),
        P(("grp", "row"), None),
    )
    return jax.shard_map(
        body,
        mesh=mesh,
        in_specs=placed,
        out_specs=(P(("grp", "row"), None), P(), P(("grp", "row"), None)),
        check_vma=False,
    )
```

```python
import functools
import math

import jax
import jax.numpy as jnp
from jax import lax
from jax.experimental import pallas as pl
from jax.experimental.pallas import tpu as pltpu
from jax.sharding import PartitionSpec as P

VMEM_LIMIT = 60 * 1024 * 1024


def silu_slope(pre):
    sigma = jax.nn.sigmoid(pre)
    return sigma * (1.0 + pre * (1.0 - sigma))


def gathered_slot(owner, q2, me):
    dk = (owner % 2) ^ (me % 2)
    rx = ((me // 2) % 4 - (owner // 2) % 4 + 4) % 4
    dy = ((owner // 8) % 2) ^ ((me // 8) % 2)
    rz = ((me // 16) - (owner // 16) + 4) % 4
    first = jnp.where(q2 == 0, rx, rz)
    second = jnp.where(q2 == 0, rz, rx)
    return (((dk * 2 + q2) * 4 + first) * 4 + second) * 2 + dy


def aggregate_kernel(me_ref, cols_ref, count_ref, vals_hbm, low_hbm, high_hbm, out_ref, vals, panel, sems):
    row_blocks, slot_total, block, _ = vals.shape
    parts, part_rows, _ = panel.shape
    col_blocks = parts * part_rows // block
    load_vals = pltpu.make_async_copy(vals_hbm, vals, sems.at[0])
    load_low = pltpu.make_async_copy(low_hbm, panel.at[0], sems.at[1])
    load_high = pltpu.make_async_copy(high_hbm, panel.at[1], sems.at[2])
    load_vals.start()
    load_low.start()
    load_high.start()
    load_vals.wait()
    load_low.wait()
    load_high.wait()
    for t in range(row_blocks):
        live = jnp.clip(count_ref[t], 0, slot_total)

        def body(k, acc):
            col = jnp.clip(cols_ref[t, k], 0, col_blocks - 1)
            owner, q = col // 4, col % 4
            place = jnp.where(q < 2, owner * 2 + q % 2, gathered_slot(owner, q % 2, me_ref[0]))
            start = pl.multiple_of(place * block, block)
            return acc + jnp.dot(
                vals[t, k], panel[q // 2, pl.ds(start, block), :], preferred_element_type=jnp.float32
            )

        out_ref[t] = lax.fori_loop(0, live, body, jnp.zeros(out_ref.shape[1:], jnp.float32))


def owner_slot(col, me, per_dev):
    owner, q = col // per_dev, col % per_dev
    dk = (owner % 2) ^ (me % 2)
    dx = ((owner // 2) % 4 - (me // 2) % 4 + 4) % 4
    dy = ((owner // 8) % 2) ^ ((me // 8) % 2)
    dz = ((owner // 16) - (me // 16) + 4) % 4
    half, q2 = q // 2, q % 2
    first = jnp.where(half == 0, dx, dz)
    second = jnp.where(half == 0, dz, dx)
    return (dk * 2 + half) * 64 + ((first * 4 + second) * 2 + dy) * 2 + q2


def spread_kernel(side_ref, cols_ref, count_ref, vals_hbm, grad_ref, keep_hbm, send_hbm, vals, total, sems):
    row_blocks, slot_total, block, _ = vals.shape
    per_panel = grad_ref.shape[1]
    col_blocks = total.shape[0]
    per_dev = col_blocks // 64
    me = side_ref[1]
    load_vals = pltpu.make_async_copy(vals_hbm, vals, sems.at[0])
    load_vals.start()

    def clear(c, carry):
        total[c] = jnp.zeros(total.shape[1:], total.dtype)
        return carry

    lax.fori_loop(0, col_blocks, clear, 0)
    load_vals.wait()
    for t in range(row_blocks):
        live = jnp.clip(count_ref[t], 0, slot_total)
        panel, within = divmod(t, per_panel)
        grad = grad_ref[jnp.where(side_ref[0] == panel, 0, 1), within]

        def body(k, carry):
            col = jnp.clip(cols_ref[t, k], 0, col_blocks - 1)
            contrib = lax.dot_general(
                vals[t, k], grad, (((0,), (0,)), ((), ())), preferred_element_type=jnp.float32
            )
            slot = owner_slot(col, me, per_dev)
            total[slot] += contrib
            return carry

        lax.fori_loop(0, live, body, 0)
    half = col_blocks // 2
    keep = pltpu.make_async_copy(total.at[pl.ds(0, half)], keep_hbm, sems.at[1])
    send = pltpu.make_async_copy(total.at[pl.ds(half, half)], send_hbm, sems.at[2])
    send.start()
    keep.start()
    send.wait()
    keep.wait()


def aggregate(me, cols, count, vals, low, high):
    row_blocks, slot_total, block, _ = vals.shape
    width = low.shape[1]
    return pl.pallas_call(
        aggregate_kernel,
        out_shape=jax.ShapeDtypeStruct((row_blocks, block, width), jnp.float32),
        in_specs=[
            pl.BlockSpec(memory_space=pltpu.SMEM),
            pl.BlockSpec(memory_space=pltpu.SMEM),
            pl.BlockSpec(memory_space=pltpu.SMEM),
            pl.BlockSpec(memory_space=pl.ANY),
            pl.BlockSpec(memory_space=pl.ANY),
            pl.BlockSpec(memory_space=pl.ANY),
        ],
        out_specs=pl.BlockSpec(memory_space=pltpu.VMEM),
        scratch_shapes=[
            pltpu.VMEM(vals.shape, vals.dtype),
            pltpu.VMEM((2, *low.shape), low.dtype),
            pltpu.SemaphoreType.DMA((3,)),
        ],
        compiler_params=pltpu.CompilerParams(vmem_limit_bytes=VMEM_LIMIT),
        cost_estimate=pl.CostEstimate(
            flops=2 * row_blocks * slot_total * block * block * width,
            bytes_accessed=vals.size * 2 + low.size * 4 + row_blocks * block * width * 4,
            transcendentals=0,
        ),
    )(me, cols, count, vals, low, high)


def spread(side, cols, count, vals, grad, col_blocks):
    row_blocks, slot_total, block, _ = vals.shape
    width = grad.shape[-1]
    return pl.pallas_call(
        spread_kernel,
        out_shape=[jax.ShapeDtypeStruct((col_blocks // 2, block, width), jnp.float32)] * 2,
        in_specs=[
            pl.BlockSpec(memory_space=pltpu.SMEM),
            pl.BlockSpec(memory_space=pltpu.SMEM),
            pl.BlockSpec(memory_space=pltpu.SMEM),
            pl.BlockSpec(memory_space=pl.ANY),
            pl.BlockSpec(memory_space=pltpu.VMEM),
        ],
        out_specs=[pl.BlockSpec(memory_space=pl.ANY)] * 2,
        scratch_shapes=[
            pltpu.VMEM(vals.shape, vals.dtype),
            pltpu.VMEM((col_blocks, block, width), jnp.float32),
            pltpu.SemaphoreType.DMA((3,)),
        ],
        compiler_params=pltpu.CompilerParams(vmem_limit_bytes=VMEM_LIMIT),
        cost_estimate=pl.CostEstimate(
            flops=2 * row_blocks * slot_total * block * block * width,
            bytes_accessed=vals.size * 2 + grad.size * 2 + col_blocks * block * width * 4,
            transcendentals=0,
        ),
    )(side, cols, count, vals, grad)


def swap(value, axis):
    size = lax.axis_size(axis)
    return lax.ppermute(value, axis, [(i, i ^ 1) for i in range(size)])


def shifted(value, digit, size, shift):
    def dest(r):
        place = (r // digit) % size
        return r + (((place + shift) % size) - place) * digit

    return lax.ppermute(value, "row", [(r, dest(r)) for r in range(64)])


def row_reduce_scatter(keep, send):
    _, block, width = keep.shape
    keep = keep.reshape(2, 4, 16, block, width)
    came = shifted(send, 1, 2, 1).reshape(2, 4, 16, block, width)
    first = [keep[0, s] + came[0, s] for s in range(4)]
    second = [keep[1, s] + came[1, s] for s in range(4)]
    first = (first[0] + sum(shifted(first[s], 2, 4, s) for s in range(1, 4))).reshape(4, 4, block, width)
    second = (second[0] + sum(shifted(second[s], 16, 4, s) for s in range(1, 4))).reshape(4, 4, block, width)
    first = (first[0] + sum(shifted(first[s], 16, 4, s) for s in range(1, 4))).reshape(2, 2, block, width)
    second = (second[0] + sum(shifted(second[s], 2, 4, s) for s in range(1, 4))).reshape(2, 2, block, width)
    first = first[0] + shifted(first[1], 8, 2, 1)
    second = second[0] + shifted(second[1], 8, 2, 1)
    return jnp.concatenate([first, second]).reshape(-1, width)


def row_all_gather(piece):
    both = jnp.stack([piece, shifted(piece, 8, 2, 1)], axis=1)
    first, second = both[0], both[1]
    first = jnp.stack([first] + [shifted(first, 16, 4, s) for s in range(1, 4)])
    second = jnp.stack([second] + [shifted(second, 2, 4, s) for s in range(1, 4)])
    first = jnp.stack([first] + [shifted(first, 2, 4, s) for s in range(1, 4)])
    second = jnp.stack([second] + [shifted(second, 16, 4, s) for s in range(1, 4)])
    mine = jnp.stack([first, second])
    whole = jnp.stack([mine, shifted(mine, 1, 2, 1)])
    return whole.reshape(-1, piece.shape[-1])


def all_sum(value, axis):
    size = lax.axis_size(axis)
    step = 1
    while step < size:
        value = value + lax.ppermute(value, axis, [(i, i ^ step) for i in range(size)])
        step *= 2
    return value


def body(features, weight, block_vals, block_cols, block_count, cotangent):
    rows_dev, width = features.shape
    block = block_vals.shape[-1]
    groups = lax.axis_size("grp")
    members = lax.axis_size("row")
    verts = rows_dev * groups * members
    side = lax.axis_index("grp")
    split = rows_dev // 2
    low = lax.all_gather(features[:split], "row", axis=0, tiled=True)
    high = row_all_gather(features[split:].reshape(2, block, width))
    col_blocks = 2 * low.shape[0] // block
    cols = block_cols[0]
    count = block_count[0]
    vals = block_vals[0]

    partial_value = aggregate(lax.axis_index("row").reshape(1).astype(jnp.int32), cols, count, vals, low, high).reshape(-1, width)
    mine = lax.dynamic_slice_in_dim(partial_value, side * rows_dev, rows_dev)
    theirs = lax.dynamic_slice_in_dim(partial_value, (1 - side) * rows_dev, rows_dev)
    summed = mine + swap(theirs, "grp")
    aggregated = summed.astype(jnp.bfloat16)
    pre = jnp.dot(aggregated, weight, preferred_element_type=jnp.float32)
    activated = jax.nn.silu(pre).astype(jnp.bfloat16)
    pre_grad = (cotangent.astype(jnp.float32) * silu_slope(pre)).astype(jnp.bfloat16)
    local_grad = jnp.dot(aggregated.T, pre_grad, preferred_element_type=jnp.float32)
    own_grad = jnp.dot(pre_grad, weight.T, preferred_element_type=jnp.float32).astype(jnp.bfloat16)
    both_grad = jnp.stack([own_grad, swap(own_grad, "grp")]).reshape(2, -1, block, width)
    weight_grad = all_sum(all_sum(local_grad, "grp"), "row")
    weight_grad, both_grad = lax.optimization_barrier((weight_grad, both_grad))
    weight_grad = weight_grad * (1.0 / math.sqrt(verts))

    where = jnp.stack([side, lax.axis_index("row")]).astype(jnp.int32)
    keep, send = spread(where, cols, count, vals, both_grad, col_blocks)
    input_grad = row_reduce_scatter(keep, send).astype(jnp.bfloat16)
    return (activated, weight_grad, input_grad)


def solution(mesh):
    placed = (
        P(("grp", "row"), None),
        P(),
        P("grp", "row", None, None, None),
        P("grp", "row", None),
        P("grp", "row"),
        P(("grp", "row"), None),
    )
    return jax.shard_map(
        body,
        mesh=mesh,
        in_specs=placed,
        out_specs=(P(("grp", "row"), None), P(), P(("grp", "row"), None)),
        check_vma=False,
    )
```

```python
import functools
import math

import jax
import jax.numpy as jnp
from jax import lax
from jax.experimental import pallas as pl
from jax.experimental.pallas import tpu as pltpu
from jax.sharding import PartitionSpec as P

VMEM_LIMIT = 60 * 1024 * 1024


def silu_slope(pre):
    sigma = jax.nn.sigmoid(pre)
    return sigma * (1.0 + pre * (1.0 - sigma))


def aggregate_kernel(cols_ref, count_ref, vals_hbm, panel_hbm, out_ref, vals, panel, sems):
    row_blocks, slot_total, block, _ = vals.shape
    col_blocks = panel.shape[0] // block
    load_vals = pltpu.make_async_copy(vals_hbm, vals, sems.at[0])
    load_panel = pltpu.make_async_copy(panel_hbm, panel, sems.at[1])
    load_vals.start()
    load_panel.start()
    load_vals.wait()
    load_panel.wait()
    for t in range(row_blocks):
        live = jnp.clip(count_ref[t], 0, slot_total)

        def body(k, acc):
            col = jnp.clip(cols_ref[t, k], 0, col_blocks - 1)
            start = pl.multiple_of(col * block, block)
            return acc + jnp.dot(
                vals[t, k], panel[pl.ds(start, block), :], preferred_element_type=jnp.float32
            )

        out_ref[t] = lax.fori_loop(0, live, body, jnp.zeros(out_ref.shape[1:], jnp.float32))


def owner_slot(col, me, per_dev):
    owner, q = col // per_dev, col % per_dev
    dk = (owner % 2) ^ (me % 2)
    dx = ((owner // 2) % 4 - (me // 2) % 4 + 4) % 4
    dy = ((owner // 8) % 2) ^ ((me // 8) % 2)
    dz = ((owner // 16) - (me // 16) + 4) % 4
    half, q2 = q // 2, q % 2
    first = jnp.where(half == 0, dx, dz)
    second = jnp.where(half == 0, dz, dx)
    return (dk * 2 + half) * 64 + ((first * 4 + second) * 2 + dy) * 2 + q2


def spread_kernel(side_ref, cols_ref, count_ref, vals_hbm, grad_ref, extra_ref, keep_hbm, send_hbm, vals, total, sems):
    row_blocks, slot_total, block, _ = vals.shape
    per_panel = grad_ref.shape[1]
    col_blocks = total.shape[0]
    per_dev = col_blocks // 64
    me = side_ref[1]
    load_vals = pltpu.make_async_copy(vals_hbm, vals, sems.at[0])
    load_vals.start()

    def clear(c, carry):
        total[c] = jnp.zeros(total.shape[1:], total.dtype)
        return carry

    lax.fori_loop(0, col_blocks, clear, 0)
    load_vals.wait()
    for t in range(row_blocks):
        live = jnp.clip(count_ref[t], 0, slot_total)
        panel, within = divmod(t, per_panel)
        grad = grad_ref[jnp.where(side_ref[0] == panel, 0, 1), within]

        def body(k, carry):
            col = jnp.clip(cols_ref[t, k], 0, col_blocks - 1)
            contrib = lax.dot_general(
                vals[t, k], grad, (((0,), (0,)), ((), ())), preferred_element_type=jnp.float32
            )
            slot = owner_slot(col, me, per_dev)
            total[slot] += contrib
            return carry

        lax.fori_loop(0, live, body, 0)
    half = col_blocks // 2
    keep = pltpu.make_async_copy(total.at[pl.ds(0, half)], keep_hbm, sems.at[1])
    send = pltpu.make_async_copy(total.at[pl.ds(half, half)], send_hbm.at[pl.ds(0, half)], sems.at[2])
    tail = pltpu.make_async_copy(extra_ref, send_hbm.at[pl.ds(half, extra_ref.shape[0])], sems.at[3])
    send.start()
    keep.start()
    tail.start()
    send.wait()
    keep.wait()
    tail.wait()


def aggregate(cols, count, vals, panel):
    row_blocks, slot_total, block, _ = vals.shape
    width = panel.shape[1]
    return pl.pallas_call(
        aggregate_kernel,
        out_shape=jax.ShapeDtypeStruct((row_blocks, block, width), jnp.float32),
        in_specs=[
            pl.BlockSpec(memory_space=pltpu.SMEM),
            pl.BlockSpec(memory_space=pltpu.SMEM),
            pl.BlockSpec(memory_space=pl.ANY),
            pl.BlockSpec(memory_space=pl.ANY),
        ],
        out_specs=pl.BlockSpec(memory_space=pltpu.VMEM),
        scratch_shapes=[
            pltpu.VMEM(vals.shape, vals.dtype),
            pltpu.VMEM(panel.shape, panel.dtype),
            pltpu.SemaphoreType.DMA((2,)),
        ],
        compiler_params=pltpu.CompilerParams(vmem_limit_bytes=VMEM_LIMIT),
        cost_estimate=pl.CostEstimate(
            flops=2 * row_blocks * slot_total * block * block * width,
            bytes_accessed=vals.size * 2 + panel.size * 2 + row_blocks * block * width * 4,
            transcendentals=0,
        ),
    )(cols, count, vals, panel)


def spread(side, cols, count, vals, grad, extra, col_blocks):
    row_blocks, slot_total, block, _ = vals.shape
    width = grad.shape[-1]
    return pl.pallas_call(
        spread_kernel,
        out_shape=[
            jax.ShapeDtypeStruct((col_blocks // 2, block, width), jnp.float32),
            jax.ShapeDtypeStruct((col_blocks // 2 + extra.shape[0], block, width), jnp.float32),
        ],
        in_specs=[
            pl.BlockSpec(memory_space=pltpu.SMEM),
            pl.BlockSpec(memory_space=pltpu.SMEM),
            pl.BlockSpec(memory_space=pltpu.SMEM),
            pl.BlockSpec(memory_space=pl.ANY),
            pl.BlockSpec(memory_space=pltpu.VMEM),
            pl.BlockSpec(memory_space=pltpu.VMEM),
        ],
        out_specs=[pl.BlockSpec(memory_space=pl.ANY)] * 2,
        scratch_shapes=[
            pltpu.VMEM(vals.shape, vals.dtype),
            pltpu.VMEM((col_blocks, block, width), jnp.float32),
            pltpu.SemaphoreType.DMA((4,)),
        ],
        compiler_params=pltpu.CompilerParams(vmem_limit_bytes=VMEM_LIMIT),
        cost_estimate=pl.CostEstimate(
            flops=2 * row_blocks * slot_total * block * block * width,
            bytes_accessed=vals.size * 2 + grad.size * 2 + col_blocks * block * width * 4,
            transcendentals=0,
        ),
    )(side, cols, count, vals, grad, extra)


def swap(value, axis):
    size = lax.axis_size(axis)
    return lax.ppermute(value, axis, [(i, i ^ 1) for i in range(size)])


def shifted(value, digit, size, shift):
    def dest(r):
        place = (r // digit) % size
        return r + (((place + shift) % size) - place) * digit

    return lax.ppermute(value, "row", [(r, dest(r)) for r in range(64)])


def ordered_sum(own, came, place, size):
    values = [own, *came]
    ordered = []
    for position in range(size):
        shift = (place - position + size) % size
        picked = values[0]
        for s in range(1, size):
            picked = jnp.where(shift == s, values[s], picked)
        ordered.append(picked)
    return (ordered[0] + ordered[1]) + (ordered[2] + ordered[3])


def row_reduce_scatter(keep, send, me):
    half, block, width = keep.shape
    extra = send.shape[0] - half
    keep = keep.reshape(2, 4, 16, block, width)
    came = shifted(send, 1, 2, 1)
    held = send[half:] + came[half:]
    came = came[:half].reshape(2, 4, 16, block, width)
    first = [keep[0, s] + came[0, s] for s in range(4)]
    second = [keep[1, s] + came[1, s] for s in range(4)]

    held = ordered_sum(held, [shifted(held, 2, 4, s) for s in range(1, 4)], (me // 2) % 4, 4)
    first = (first[0] + sum(shifted(first[s], 2, 4, s) for s in range(1, 4))).reshape(4, 4, block, width)
    second = (second[0] + sum(shifted(second[s], 16, 4, s) for s in range(1, 4))).reshape(4, 4, block, width)

    held = ordered_sum(held, [shifted(held, 16, 4, s) for s in range(1, 4)], me // 16, 4)
    first = (first[0] + sum(shifted(first[s], 16, 4, s) for s in range(1, 4))).reshape(2, 2, block, width)
    second = (second[0] + sum(shifted(second[s], 2, 4, s) for s in range(1, 4))).reshape(2, 2, block, width)

    held = held + shifted(held, 8, 2, 1)
    first = first[0] + shifted(first[1], 8, 2, 1)
    second = second[0] + shifted(second[1], 8, 2, 1)
    return jnp.concatenate([first, second]).reshape(-1, width), held


def all_sum(value, axis):
    size = lax.axis_size(axis)
    step = 1
    while step < size:
        value = value + lax.ppermute(value, axis, [(i, i ^ step) for i in range(size)])
        step *= 2
    return value


def body(features, weight, block_vals, block_cols, block_count, cotangent):
    rows_dev, width = features.shape
    block = block_vals.shape[-1]
    groups = lax.axis_size("grp")
    members = lax.axis_size("row")
    verts = rows_dev * groups * members
    side = lax.axis_index("grp")
    gathered = lax.all_gather(features, "row", axis=0, tiled=True)
    col_blocks = gathered.shape[0] // block
    cols = block_cols[0]
    count = block_count[0]
    vals = block_vals[0]

    partial_value = aggregate(cols, count, vals, gathered).reshape(-1, width)
    mine = lax.dynamic_slice_in_dim(partial_value, side * rows_dev, rows_dev)
    theirs = lax.dynamic_slice_in_dim(partial_value, (1 - side) * rows_dev, rows_dev)
    summed = mine + swap(theirs, "grp")
    aggregated = summed.astype(jnp.bfloat16)
    pre = jnp.dot(aggregated, weight, preferred_element_type=jnp.float32)
    activated = jax.nn.silu(pre).astype(jnp.bfloat16)
    pre_grad = (cotangent.astype(jnp.float32) * silu_slope(pre)).astype(jnp.bfloat16)
    local_grad = jnp.dot(aggregated.T, pre_grad, preferred_element_type=jnp.float32)
    own_grad = jnp.dot(pre_grad, weight.T, preferred_element_type=jnp.float32).astype(jnp.bfloat16)
    both_grad = jnp.stack([own_grad, swap(own_grad, "grp")]).reshape(2, -1, block, width)

    where = jnp.stack([side, lax.axis_index("row")]).astype(jnp.int32)
    extra = local_grad.reshape(-1, block, width)
    keep, send = spread(where, cols, count, vals, both_grad, extra, col_blocks)
    input_grad, held = row_reduce_scatter(keep, send, lax.axis_index("row"))
    input_grad = input_grad.astype(jnp.bfloat16)
    held = held.reshape(-1, width)
    weight_grad = (held + swap(held, "grp")) * (1.0 / math.sqrt(verts))
    return (activated, weight_grad, input_grad)


def solution(mesh):
    placed = (
        P(("grp", "row"), None),
        P(),
        P("grp", "row", None, None, None),
        P("grp", "row", None),
        P("grp", "row"),
        P(("grp", "row"), None),
    )
    return jax.shard_map(
        body,
        mesh=mesh,
        in_specs=placed,
        out_specs=(P(("grp", "row"), None), P(), P(("grp", "row"), None)),
        check_vma=False,
    )
```

```python
import functools
import itertools
import math

import jax
import jax.numpy as jnp
from jax import lax
from jax.experimental import pallas as pl
from jax.experimental.pallas import tpu as pltpu
from jax.sharding import PartitionSpec as P

VMEM_LIMIT = 60 * 1024 * 1024


def silu_slope(pre):
    sigma = jax.nn.sigmoid(pre)
    return sigma * (1.0 + pre * (1.0 - sigma))


def aggregate_kernel(cols_ref, count_ref, vals_hbm, panel_hbm, out_ref, vals, panel, sems):
    row_blocks, slot_total, block, _ = vals.shape
    col_blocks = panel.shape[0] // block
    load_vals = pltpu.make_async_copy(vals_hbm, vals, sems.at[0])
    load_panel = pltpu.make_async_copy(panel_hbm, panel, sems.at[1])
    load_vals.start()
    load_panel.start()
    load_vals.wait()
    load_panel.wait()
    for t in range(row_blocks):
        live = jnp.clip(count_ref[t], 0, slot_total)

        def body(k, acc):
            col = jnp.clip(cols_ref[t, k], 0, col_blocks - 1)
            start = pl.multiple_of(col * block, block)
            return acc + jnp.dot(
                vals[t, k], panel[pl.ds(start, block), :], preferred_element_type=jnp.float32
            )

        out_ref[t] = lax.fori_loop(0, live, body, jnp.zeros(out_ref.shape[1:], jnp.float32))


def owner_slot(col, me, per_dev):
    owner, q = col // per_dev, col % per_dev
    dk = (owner % 2) ^ (me % 2)
    dx = ((owner // 2) % 4 - (me // 2) % 4 + 4) % 4
    dy = ((owner // 8) % 2) ^ ((me // 8) % 2)
    dz = ((owner // 16) - (me // 16) + 4) % 4
    half, q2 = q // 2, q % 2
    first = jnp.where(half == 0, dx, dz)
    second = jnp.where(half == 0, dz, dx)
    return (dk * 2 + half) * 64 + ((first * 4 + second) * 2 + dy) * 2 + q2


def spread_kernel(side_ref, cols_ref, count_ref, vals_hbm, grad_ref, keep_hbm, send_hbm, vals, total, sems):
    row_blocks, slot_total, block, _ = vals.shape
    per_panel = grad_ref.shape[1]
    col_blocks = total.shape[0]
    per_dev = col_blocks // 64
    me = side_ref[1]
    load_vals = pltpu.make_async_copy(vals_hbm, vals, sems.at[0])
    load_vals.start()

    def clear(c, carry):
        total[c] = jnp.zeros(total.shape[1:], total.dtype)
        return carry

    lax.fori_loop(0, col_blocks, clear, 0)
    load_vals.wait()
    for t in range(row_blocks):
        live = jnp.clip(count_ref[t], 0, slot_total)
        panel, within = divmod(t, per_panel)
        grad = grad_ref[jnp.where(side_ref[0] == panel, 0, 1), within]

        def body(k, carry):
            col = jnp.clip(cols_ref[t, k], 0, col_blocks - 1)
            contrib = lax.dot_general(
                vals[t, k], grad, (((0,), (0,)), ((), ())), preferred_element_type=jnp.float32
            )
            slot = owner_slot(col, me, per_dev)
            total[slot] += contrib
            return carry

        lax.fori_loop(0, live, body, 0)
    half = col_blocks // 2
    keep = pltpu.make_async_copy(total.at[pl.ds(0, half)], keep_hbm, sems.at[1])
    send = pltpu.make_async_copy(total.at[pl.ds(half, half)], send_hbm, sems.at[2])
    send.start()
    keep.start()
    send.wait()
    keep.wait()


def aggregate(cols, count, vals, panel):
    row_blocks, slot_total, block, _ = vals.shape
    width = panel.shape[1]
    return pl.pallas_call(
        aggregate_kernel,
        out_shape=jax.ShapeDtypeStruct((row_blocks, block, width), jnp.float32),
        in_specs=[
            pl.BlockSpec(memory_space=pltpu.SMEM),
            pl.BlockSpec(memory_space=pltpu.SMEM),
            pl.BlockSpec(memory_space=pl.ANY),
            pl.BlockSpec(memory_space=pl.ANY),
        ],
        out_specs=pl.BlockSpec(memory_space=pltpu.VMEM),
        scratch_shapes=[
            pltpu.VMEM(vals.shape, vals.dtype),
            pltpu.VMEM(panel.shape, panel.dtype),
            pltpu.SemaphoreType.DMA((2,)),
        ],
        compiler_params=pltpu.CompilerParams(vmem_limit_bytes=VMEM_LIMIT),
        cost_estimate=pl.CostEstimate(
            flops=2 * row_blocks * slot_total * block * block * width,
            bytes_accessed=vals.size * 2 + panel.size * 2 + row_blocks * block * width * 4,
            transcendentals=0,
        ),
    )(cols, count, vals, panel)


def spread(side, cols, count, vals, grad, col_blocks):
    row_blocks, slot_total, block, _ = vals.shape
    width = grad.shape[-1]
    return pl.pallas_call(
        spread_kernel,
        out_shape=[jax.ShapeDtypeStruct((col_blocks // 2, block, width), jnp.float32)] * 2,
        in_specs=[
            pl.BlockSpec(memory_space=pltpu.SMEM),
            pl.BlockSpec(memory_space=pltpu.SMEM),
            pl.BlockSpec(memory_space=pltpu.SMEM),
            pl.BlockSpec(memory_space=pl.ANY),
            pl.BlockSpec(memory_space=pltpu.VMEM),
        ],
        out_specs=[pl.BlockSpec(memory_space=pl.ANY)] * 2,
        scratch_shapes=[
            pltpu.VMEM(vals.shape, vals.dtype),
            pltpu.VMEM((col_blocks, block, width), jnp.float32),
            pltpu.SemaphoreType.DMA((3,)),
        ],
        compiler_params=pltpu.CompilerParams(vmem_limit_bytes=VMEM_LIMIT),
        cost_estimate=pl.CostEstimate(
            flops=2 * row_blocks * slot_total * block * block * width,
            bytes_accessed=vals.size * 2 + grad.size * 2 + col_blocks * block * width * 4,
            transcendentals=0,
        ),
    )(side, cols, count, vals, grad)


def swap(value, axis):
    size = lax.axis_size(axis)
    return lax.ppermute(value, axis, [(i, i ^ 1) for i in range(size)])


def shifted(value, digit, size, shift):
    def dest(r):
        place = (r // digit) % size
        return r + (((place + shift) % size) - place) * digit

    return lax.ppermute(value, "row", [(r, dest(r)) for r in range(64)])


def row_reduce_scatter(keep, send):
    _, block, width = keep.shape
    keep = keep.reshape(2, 4, 16, block, width)
    came = shifted(send, 1, 2, 1).reshape(2, 4, 16, block, width)
    first = [keep[0, s] + came[0, s] for s in range(4)]
    second = [keep[1, s] + came[1, s] for s in range(4)]
    first = (first[0] + sum(shifted(first[s], 2, 4, s) for s in range(1, 4))).reshape(4, 4, block, width)
    second = (second[0] + sum(shifted(second[s], 16, 4, s) for s in range(1, 4))).reshape(4, 4, block, width)
    first = (first[0] + sum(shifted(first[s], 16, 4, s) for s in range(1, 4))).reshape(2, 2, block, width)
    second = (second[0] + sum(shifted(second[s], 2, 4, s) for s in range(1, 4))).reshape(2, 2, block, width)
    first = first[0] + shifted(first[1], 8, 2, 1)
    second = second[0] + shifted(second[1], 8, 2, 1)
    return jnp.concatenate([first, second]).reshape(-1, width)


def group_sum(value, axes, digits):
    size_all = 1
    for axis in axes:
        size_all *= lax.axis_size(axis)
    me = lax.axis_index(axes)
    combos = list(itertools.product(*[range(size) for _, size in digits]))
    came = [value]
    for combo in combos[1:]:
        pairs = []
        for r in range(size_all):
            dest = r
            for (digit, size), shift in zip(digits, combo):
                place = (r // digit) % size
                dest += (((place + shift) % size) - place) * digit
            pairs.append((r, dest))
        came.append(lax.ppermute(value, axes, pairs))
    ordered = []
    for target in combos:
        code = 0
        for (digit, size), spot in zip(digits, target):
            code = code * size + ((me // digit) % size - spot + size) % size
        picked = came[0]
        for index in range(1, len(combos)):
            picked = jnp.where(code == index, came[index], picked)
        ordered.append(picked)
    while len(ordered) > 1:
        ordered = [ordered[i] + ordered[i + 1] for i in range(0, len(ordered), 2)]
    return ordered[0]


def all_sum(value, axis):
    size = lax.axis_size(axis)
    step = 1
    while step < size:
        value = value + lax.ppermute(value, axis, [(i, i ^ step) for i in range(size)])
        step *= 2
    return value


def body(features, weight, block_vals, block_cols, block_count, cotangent):
    rows_dev, width = features.shape
    block = block_vals.shape[-1]
    groups = lax.axis_size("grp")
    members = lax.axis_size("row")
    verts = rows_dev * groups * members
    side = lax.axis_index("grp")
    gathered = lax.all_gather(features, "row", axis=0, tiled=True)
    col_blocks = gathered.shape[0] // block
    cols = block_cols[0]
    count = block_count[0]
    vals = block_vals[0]

    partial_value = aggregate(cols, count, vals, gathered).reshape(-1, width)
    mine = lax.dynamic_slice_in_dim(partial_value, side * rows_dev, rows_dev)
    theirs = lax.dynamic_slice_in_dim(partial_value, (1 - side) * rows_dev, rows_dev)
    summed = mine + swap(theirs, "grp")
    aggregated = summed.astype(jnp.bfloat16)
    pre = jnp.dot(aggregated, weight, preferred_element_type=jnp.float32)
    activated = jax.nn.silu(pre).astype(jnp.bfloat16)
    pre_grad = (cotangent.astype(jnp.float32) * silu_slope(pre)).astype(jnp.bfloat16)
    local_grad = jnp.dot(aggregated.T, pre_grad, preferred_element_type=jnp.float32)
    own_grad = jnp.dot(pre_grad, weight.T, preferred_element_type=jnp.float32).astype(jnp.bfloat16)
    both_grad = jnp.stack([own_grad, swap(own_grad, "grp")]).reshape(2, -1, block, width)
    weight_grad = group_sum(local_grad, ("row",), [(2, 4), (1, 2)])
    weight_grad = group_sum(weight_grad, ("row",), [(16, 4)])
    weight_grad = group_sum(weight_grad, ("grp", "row"), [(64, 2), (8, 2)])
    weight_grad, both_grad = lax.optimization_barrier((weight_grad, both_grad))
    weight_grad = weight_grad * (1.0 / math.sqrt(verts))

    where = jnp.stack([side, lax.axis_index("row")]).astype(jnp.int32)
    keep, send = spread(where, cols, count, vals, both_grad, col_blocks)
    input_grad = row_reduce_scatter(keep, send).astype(jnp.bfloat16)
    return (activated, weight_grad, input_grad)


def solution(mesh):
    placed = (
        P(("grp", "row"), None),
        P(),
        P("grp", "row", None, None, None),
        P("grp", "row", None),
        P("grp", "row"),
        P(("grp", "row"), None),
    )
    return jax.shard_map(
        body,
        mesh=mesh,
        in_specs=placed,
        out_specs=(P(("grp", "row"), None), P(), P(("grp", "row"), None)),
        check_vma=False,
    )
```

```python
import functools
import math

import jax
import jax.numpy as jnp
from jax import lax
from jax.experimental import pallas as pl
from jax.experimental.pallas import tpu as pltpu
from jax.sharding import PartitionSpec as P

VMEM_LIMIT = 60 * 1024 * 1024


def silu_slope(pre):
    sigma = jax.nn.sigmoid(pre)
    return sigma * (1.0 + pre * (1.0 - sigma))


def aggregate_kernel(cols_ref, count_ref, vals_hbm, panel_hbm, out_ref, vals, panel, sems):
    row_blocks, slot_total, block, _ = vals.shape
    col_blocks = panel.shape[0] // block
    load_vals = pltpu.make_async_copy(vals_hbm, vals, sems.at[0])
    load_panel = pltpu.make_async_copy(panel_hbm, panel, sems.at[1])
    load_vals.start()
    load_panel.start()
    load_vals.wait()
    load_panel.wait()
    for t in range(row_blocks):
        live = jnp.clip(count_ref[t], 0, slot_total)

        acc = jnp.zeros(out_ref.shape[1:], jnp.float32)
        for k in range(slot_total):
            col = jnp.clip(cols_ref[t, k], 0, col_blocks - 1)
            start = pl.multiple_of(col * block, block)
            picked = jnp.where(k < live, vals[t, k], jnp.zeros_like(vals[t, k]))
            acc = acc + jnp.dot(picked, panel[pl.ds(start, block), :], preferred_element_type=jnp.float32)
        out_ref[t] = acc


def owner_slot(col, me, per_dev):
    owner, q = col // per_dev, col % per_dev
    dk = (owner % 2) ^ (me % 2)
    dx = ((owner // 2) % 4 - (me // 2) % 4 + 4) % 4
    dy = ((owner // 8) % 2) ^ ((me // 8) % 2)
    dz = ((owner // 16) - (me // 16) + 4) % 4
    half, q2 = q // 2, q % 2
    first = jnp.where(half == 0, dx, dz)
    second = jnp.where(half == 0, dz, dx)
    return (dk * 2 + half) * 64 + ((first * 4 + second) * 2 + dy) * 2 + q2


def spread_kernel(side_ref, cols_ref, count_ref, vals_hbm, grad_ref, keep_hbm, send_hbm, vals, total, sems):
    row_blocks, slot_total, block, _ = vals.shape
    per_panel = grad_ref.shape[1]
    col_blocks = total.shape[0]
    per_dev = col_blocks // 64
    me = side_ref[1]
    load_vals = pltpu.make_async_copy(vals_hbm, vals, sems.at[0])
    load_vals.start()

    def clear(c, carry):
        total[c] = jnp.zeros(total.shape[1:], total.dtype)
        return carry

    lax.fori_loop(0, col_blocks, clear, 0)
    load_vals.wait()
    for t in range(row_blocks):
        live = jnp.clip(count_ref[t], 0, slot_total)
        panel, within = divmod(t, per_panel)
        grad = grad_ref[jnp.where(side_ref[0] == panel, 0, 1), within]

        for k in range(slot_total):
            col = jnp.clip(cols_ref[t, k], 0, col_blocks - 1)
            picked = jnp.where(k < live, vals[t, k], jnp.zeros_like(vals[t, k]))
            contrib = jnp.dot(picked, grad, preferred_element_type=jnp.float32)
            slot = owner_slot(col, me, per_dev)
            total[slot] += contrib
    half = col_blocks // 2
    keep = pltpu.make_async_copy(total.at[pl.ds(0, half)], keep_hbm, sems.at[1])
    send = pltpu.make_async_copy(total.at[pl.ds(half, half)], send_hbm, sems.at[2])
    send.start()
    keep.start()
    send.wait()
    keep.wait()


def aggregate(cols, count, vals, panel):
    row_blocks, slot_total, block, _ = vals.shape
    width = panel.shape[1]
    return pl.pallas_call(
        aggregate_kernel,
        out_shape=jax.ShapeDtypeStruct((row_blocks, block, width), jnp.float32),
        in_specs=[
            pl.BlockSpec(memory_space=pltpu.SMEM),
            pl.BlockSpec(memory_space=pltpu.SMEM),
            pl.BlockSpec(memory_space=pl.ANY),
            pl.BlockSpec(memory_space=pl.ANY),
        ],
        out_specs=pl.BlockSpec(memory_space=pltpu.VMEM),
        scratch_shapes=[
            pltpu.VMEM(vals.shape, vals.dtype),
            pltpu.VMEM(panel.shape, panel.dtype),
            pltpu.SemaphoreType.DMA((2,)),
        ],
        compiler_params=pltpu.CompilerParams(vmem_limit_bytes=VMEM_LIMIT),
        cost_estimate=pl.CostEstimate(
            flops=2 * row_blocks * slot_total * block * block * width,
            bytes_accessed=vals.size * 2 + panel.size * 2 + row_blocks * block * width * 4,
            transcendentals=0,
        ),
    )(cols, count, vals, panel)


def spread(side, cols, count, vals, grad, col_blocks):
    row_blocks, slot_total, block, _ = vals.shape
    width = grad.shape[-1]
    return pl.pallas_call(
        spread_kernel,
        out_shape=[jax.ShapeDtypeStruct((col_blocks // 2, block, width), jnp.float32)] * 2,
        in_specs=[
            pl.BlockSpec(memory_space=pltpu.SMEM),
            pl.BlockSpec(memory_space=pltpu.SMEM),
            pl.BlockSpec(memory_space=pltpu.SMEM),
            pl.BlockSpec(memory_space=pl.ANY),
            pl.BlockSpec(memory_space=pltpu.VMEM),
        ],
        out_specs=[pl.BlockSpec(memory_space=pl.ANY)] * 2,
        scratch_shapes=[
            pltpu.VMEM(vals.shape, vals.dtype),
            pltpu.VMEM((col_blocks, block, width), jnp.float32),
            pltpu.SemaphoreType.DMA((3,)),
        ],
        compiler_params=pltpu.CompilerParams(vmem_limit_bytes=VMEM_LIMIT),
        cost_estimate=pl.CostEstimate(
            flops=2 * row_blocks * slot_total * block * block * width,
            bytes_accessed=vals.size * 2 + grad.size * 2 + col_blocks * block * width * 4,
            transcendentals=0,
        ),
    )(side, cols, count, vals, grad)


def swap(value, axis):
    size = lax.axis_size(axis)
    return lax.ppermute(value, axis, [(i, i ^ 1) for i in range(size)])


def shifted(value, digit, size, shift):
    def dest(r):
        place = (r // digit) % size
        return r + (((place + shift) % size) - place) * digit

    return lax.ppermute(value, "row", [(r, dest(r)) for r in range(64)])


def row_reduce_scatter(keep, send):
    _, block, width = keep.shape
    keep = keep.reshape(2, 4, 16, block, width)
    came = shifted(send, 1, 2, 1).reshape(2, 4, 16, block, width)
    first = [keep[0, s] + came[0, s] for s in range(4)]
    second = [keep[1, s] + came[1, s] for s in range(4)]
    first = (first[0] + sum(shifted(first[s], 2, 4, s) for s in range(1, 4))).reshape(4, 4, block, width)
    second = (second[0] + sum(shifted(second[s], 16, 4, s) for s in range(1, 4))).reshape(4, 4, block, width)
    first = (first[0] + sum(shifted(first[s], 16, 4, s) for s in range(1, 4))).reshape(2, 2, block, width)
    second = (second[0] + sum(shifted(second[s], 2, 4, s) for s in range(1, 4))).reshape(2, 2, block, width)
    first = first[0] + shifted(first[1], 8, 2, 1)
    second = second[0] + shifted(second[1], 8, 2, 1)
    return jnp.concatenate([first, second]).reshape(-1, width)


def all_sum(value, axis):
    size = lax.axis_size(axis)
    step = 1
    while step < size:
        value = value + lax.ppermute(value, axis, [(i, i ^ step) for i in range(size)])
        step *= 2
    return value


def body(features, weight, block_vals, block_cols, block_count, cotangent):
    rows_dev, width = features.shape
    block = block_vals.shape[-1]
    groups = lax.axis_size("grp")
    members = lax.axis_size("row")
    verts = rows_dev * groups * members
    side = lax.axis_index("grp")
    gathered = lax.all_gather(features, "row", axis=0, tiled=True)
    col_blocks = gathered.shape[0] // block
    cols = block_cols[0]
    count = block_count[0]
    vals = block_vals[0]

    partial_value = aggregate(cols, count, vals, gathered).reshape(-1, width)
    mine = lax.dynamic_slice_in_dim(partial_value, side * rows_dev, rows_dev)
    theirs = lax.dynamic_slice_in_dim(partial_value, (1 - side) * rows_dev, rows_dev)
    summed = mine + swap(theirs, "grp")
    aggregated = summed.astype(jnp.bfloat16)
    pre = jnp.dot(aggregated, weight, preferred_element_type=jnp.float32)
    activated = jax.nn.silu(pre).astype(jnp.bfloat16)
    pre_grad = (cotangent.astype(jnp.float32) * silu_slope(pre)).astype(jnp.bfloat16)
    local_grad = jnp.dot(aggregated.T, pre_grad, preferred_element_type=jnp.float32)
    own_grad = jnp.dot(pre_grad, weight.T, preferred_element_type=jnp.float32).astype(jnp.bfloat16)
    both_grad = jnp.stack([own_grad, swap(own_grad, "grp")]).reshape(2, -1, block, width)
    weight_grad = all_sum(all_sum(local_grad, "grp"), "row")
    weight_grad, both_grad = lax.optimization_barrier((weight_grad, both_grad))
    weight_grad = weight_grad * (1.0 / math.sqrt(verts))

    where = jnp.stack([side, lax.axis_index("row")]).astype(jnp.int32)
    keep, send = spread(where, cols, count, jnp.swapaxes(vals, 2, 3), both_grad, col_blocks)
    input_grad = row_reduce_scatter(keep, send).astype(jnp.bfloat16)
    return (activated, weight_grad, input_grad)


def solution(mesh):
    placed = (
        P(("grp", "row"), None),
        P(),
        P("grp", "row", None, None, None),
        P("grp", "row", None),
        P("grp", "row"),
        P(("grp", "row"), None),
    )
    return jax.shard_map(
        body,
        mesh=mesh,
        in_specs=placed,
        out_specs=(P(("grp", "row"), None), P(), P(("grp", "row"), None)),
        check_vma=False,
    )
```

```python
import functools
import math

import jax
import jax.numpy as jnp
from jax import lax
from jax.experimental import pallas as pl
from jax.experimental.pallas import tpu as pltpu
from jax.sharding import PartitionSpec as P

VMEM_LIMIT = 60 * 1024 * 1024


def silu_slope(pre):
    sigma = jax.nn.sigmoid(pre)
    return sigma * (1.0 + pre * (1.0 - sigma))


def aggregate_kernel(cols_ref, count_ref, vals_hbm, panel_hbm, out_ref, vals, panel, sems):
    row_blocks, slot_total, block, _ = vals.shape
    col_blocks = panel.shape[0] // block
    load_vals = pltpu.make_async_copy(vals_hbm, vals, sems.at[0])
    load_panel = pltpu.make_async_copy(panel_hbm, panel, sems.at[1])
    load_vals.start()
    load_panel.start()
    load_vals.wait()
    load_panel.wait()
    for t in range(row_blocks):
        live = jnp.clip(count_ref[t], 0, slot_total)

        acc = jnp.zeros(out_ref.shape[1:], jnp.float32)
        for k in range(slot_total):
            col = jnp.clip(cols_ref[t, k], 0, col_blocks - 1)
            start = pl.multiple_of(col * block, block)
            picked = jnp.where(k < live, vals[t, k], jnp.zeros_like(vals[t, k]))
            acc = acc + jnp.dot(picked, panel[pl.ds(start, block), :], preferred_element_type=jnp.float32)
        out_ref[t] = acc


def owner_slot(col, me, per_dev):
    owner, q = col // per_dev, col % per_dev
    dk = (owner % 2) ^ (me % 2)
    dx = ((owner // 2) % 4 - (me // 2) % 4 + 4) % 4
    dy = ((owner // 8) % 2) ^ ((me // 8) % 2)
    dz = ((owner // 16) - (me // 16) + 4) % 4
    half, q2 = q // 2, q % 2
    first = jnp.where(half == 0, dx, dz)
    second = jnp.where(half == 0, dz, dx)
    return (dk * 2 + half) * 64 + ((first * 4 + second) * 2 + dy) * 2 + q2


def spread_kernel(side_ref, cols_ref, count_ref, vals_hbm, grad_ref, *rest):
    outs, (vals, total, sems) = rest[:-3], rest[-3:]
    sources, row_blocks, slot_total, block, _ = vals.shape
    per_panel = grad_ref.shape[2]
    kept = total.shape[0]
    col_blocks = 2 * kept
    per_dev = col_blocks // 64
    me = side_ref[1]
    load_vals = pltpu.make_async_copy(vals_hbm, vals, sems.at[0])
    load_vals.start()

    def clear(c, carry):
        total[c] = jnp.zeros(total.shape[1:], total.dtype)
        return carry

    lax.fori_loop(0, kept, clear, 0)
    load_vals.wait()
    for src in range(sources):

        def row_block(t, carry):
            live = jnp.clip(count_ref[src, t], 0, slot_total)
            panel, within = t // per_panel, t % per_panel
            grad = grad_ref[src, jnp.where(side_ref[0] == panel, 0, 1), within]
            for k in range(slot_total):
                col = jnp.clip(cols_ref[src, t, k], 0, col_blocks - 1)
                slot = owner_slot(col, me, per_dev)

                @pl.when((k < live) & (slot < kept))
                def _():
                    contrib = jnp.dot(vals[src, t, k], grad, preferred_element_type=jnp.float32)
                    total[jnp.minimum(slot, kept - 1)] += contrib

            return carry

        lax.fori_loop(0, row_blocks, row_block, 0)

    chunk = kept // len(outs)
    copies = [
        pltpu.make_async_copy(total.at[pl.ds(i * chunk, chunk)], out, sems.at[1 + i])
        for i, out in enumerate(outs)
    ]
    for copy in copies:
        copy.start()
    for copy in copies:
        copy.wait()


def aggregate(cols, count, vals, panel):
    row_blocks, slot_total, block, _ = vals.shape
    width = panel.shape[1]
    return pl.pallas_call(
        aggregate_kernel,
        out_shape=jax.ShapeDtypeStruct((row_blocks, block, width), jnp.float32),
        in_specs=[
            pl.BlockSpec(memory_space=pltpu.SMEM),
            pl.BlockSpec(memory_space=pltpu.SMEM),
            pl.BlockSpec(memory_space=pl.ANY),
            pl.BlockSpec(memory_space=pl.ANY),
        ],
        out_specs=pl.BlockSpec(memory_space=pltpu.VMEM),
        scratch_shapes=[
            pltpu.VMEM(vals.shape, vals.dtype),
            pltpu.VMEM(panel.shape, panel.dtype),
            pltpu.SemaphoreType.DMA((2,)),
        ],
        compiler_params=pltpu.CompilerParams(vmem_limit_bytes=VMEM_LIMIT),
        cost_estimate=pl.CostEstimate(
            flops=2 * row_blocks * slot_total * block * block * width,
            bytes_accessed=vals.size * 2 + panel.size * 2 + row_blocks * block * width * 4,
            transcendentals=0,
        ),
    )(cols, count, vals, panel)


def spread(side, cols, count, vals, grad, col_blocks):
    sources, row_blocks, slot_total, block, _ = vals.shape
    width = grad.shape[-1]
    kept = col_blocks // 2
    pieces = 8
    return pl.pallas_call(
        spread_kernel,
        out_shape=[jax.ShapeDtypeStruct((kept // pieces, block, width), jnp.float32)] * pieces,
        in_specs=[
            pl.BlockSpec(memory_space=pltpu.SMEM),
            pl.BlockSpec(memory_space=pltpu.SMEM),
            pl.BlockSpec(memory_space=pltpu.SMEM),
            pl.BlockSpec(memory_space=pl.ANY),
            pl.BlockSpec(memory_space=pltpu.VMEM),
        ],
        out_specs=[pl.BlockSpec(memory_space=pl.ANY)] * pieces,
        scratch_shapes=[
            pltpu.VMEM(vals.shape, vals.dtype),
            pltpu.VMEM((kept, block, width), jnp.float32),
            pltpu.SemaphoreType.DMA((1 + pieces,)),
        ],
        compiler_params=pltpu.CompilerParams(vmem_limit_bytes=VMEM_LIMIT),
        cost_estimate=pl.CostEstimate(
            flops=sources * row_blocks * slot_total * block * block * width,
            bytes_accessed=vals.size * 2 + grad.size * 2 + kept * block * width * 4,
            transcendentals=0,
        ),
    )(side, cols, count, vals, grad)


def swap(value, axis):
    size = lax.axis_size(axis)
    return lax.ppermute(value, axis, [(i, i ^ 1) for i in range(size)])


def shifted(value, digit, size, shift):
    def dest(r):
        place = (r // digit) % size
        return r + (((place + shift) % size) - place) * digit

    return lax.ppermute(value, "row", [(r, dest(r)) for r in range(64)])


def row_reduce_scatter(pieces):
    _, block, width = pieces[0].shape
    first, second = pieces[:4], pieces[4:]
    first = (first[0] + sum(shifted(first[s], 2, 4, s) for s in range(1, 4))).reshape(4, 4, block, width)
    second = (second[0] + sum(shifted(second[s], 16, 4, s) for s in range(1, 4))).reshape(4, 4, block, width)
    first = (first[0] + sum(shifted(first[s], 16, 4, s) for s in range(1, 4))).reshape(2, 2, block, width)
    second = (second[0] + sum(shifted(second[s], 2, 4, s) for s in range(1, 4))).reshape(2, 2, block, width)
    first = first[0] + shifted(first[1], 8, 2, 1)
    second = second[0] + shifted(second[1], 8, 2, 1)
    return jnp.concatenate([first, second]).reshape(-1, width)


def all_sum(value, axis):
    size = lax.axis_size(axis)
    step = 1
    while step < size:
        value = value + lax.ppermute(value, axis, [(i, i ^ step) for i in range(size)])
        step *= 2
    return value


def body(features, weight, block_vals, block_cols, block_count, cotangent):
    rows_dev, width = features.shape
    block = block_vals.shape[-1]
    groups = lax.axis_size("grp")
    members = lax.axis_size("row")
    verts = rows_dev * groups * members
    side = lax.axis_index("grp")
    gathered = lax.all_gather(features, "row", axis=0, tiled=True)
    col_blocks = gathered.shape[0] // block
    cols = block_cols[0]
    count = block_count[0]
    vals = block_vals[0]
    chip_vals = jnp.swapaxes(vals, 2, 3)
    chip_vals = jnp.stack([chip_vals, shifted(chip_vals, 1, 2, 1)])
    chip_vals, gathered = lax.optimization_barrier((chip_vals, gathered))

    partial_value = aggregate(cols, count, vals, gathered).reshape(-1, width)
    mine = lax.dynamic_slice_in_dim(partial_value, side * rows_dev, rows_dev)
    theirs = lax.dynamic_slice_in_dim(partial_value, (1 - side) * rows_dev, rows_dev)
    summed = mine + swap(theirs, "grp")
    aggregated = summed.astype(jnp.bfloat16)
    pre = jnp.dot(aggregated, weight, preferred_element_type=jnp.float32)
    activated = jax.nn.silu(pre).astype(jnp.bfloat16)
    pre_grad = (cotangent.astype(jnp.float32) * silu_slope(pre)).astype(jnp.bfloat16)
    local_grad = jnp.dot(aggregated.T, pre_grad, preferred_element_type=jnp.float32)
    own_grad = jnp.dot(pre_grad, weight.T, preferred_element_type=jnp.float32).astype(jnp.bfloat16)
    both_grad = jnp.stack([own_grad, swap(own_grad, "grp")]).reshape(2, -1, block, width)
    weight_grad = all_sum(all_sum(local_grad, "grp"), "row")
    weight_grad, both_grad = lax.optimization_barrier((weight_grad, both_grad))
    weight_grad = weight_grad * (1.0 / math.sqrt(verts))

    where = jnp.stack([side, lax.axis_index("row")]).astype(jnp.int32)
    pair = lambda value: jnp.stack([value, shifted(value, 1, 2, 1)])
    pieces = spread(where, pair(cols), pair(count), chip_vals, pair(both_grad), col_blocks)
    input_grad = row_reduce_scatter(pieces).astype(jnp.bfloat16)
    return (activated, weight_grad, input_grad)


def solution(mesh):
    placed = (
        P(("grp", "row"), None),
        P(),
        P("grp", "row", None, None, None),
        P("grp", "row", None),
        P("grp", "row"),
        P(("grp", "row"), None),
    )
    return jax.shard_map(
        body,
        mesh=mesh,
        in_specs=placed,
        out_specs=(P(("grp", "row"), None), P(), P(("grp", "row"), None)),
        check_vma=False,
    )
```

```python
import functools
import math

import jax
import jax.numpy as jnp
from jax import lax
from jax.experimental import pallas as pl
from jax.experimental.pallas import tpu as pltpu
from jax.sharding import PartitionSpec as P

VMEM_LIMIT = 60 * 1024 * 1024


def silu_slope(pre):
    sigma = jax.nn.sigmoid(pre)
    return sigma * (1.0 + pre * (1.0 - sigma))


def aggregate_kernel(cols_ref, count_ref, vals_hbm, panel_hbm, out_ref, vals, panel, sems):
    row_blocks, slot_total, block, _ = vals.shape
    col_blocks = panel.shape[0] // block
    load_vals = pltpu.make_async_copy(vals_hbm, vals, sems.at[0])
    load_panel = pltpu.make_async_copy(panel_hbm, panel, sems.at[1])
    load_vals.start()
    load_panel.start()
    load_vals.wait()
    load_panel.wait()
    for t in range(row_blocks):
        live = jnp.clip(count_ref[t], 0, slot_total)

        acc = jnp.zeros(out_ref.shape[1:], jnp.float32)
        for k in range(slot_total):
            col = jnp.clip(cols_ref[t, k], 0, col_blocks - 1)
            start = pl.multiple_of(col * block, block)
            picked = jnp.where(k < live, vals[t, k], jnp.zeros_like(vals[t, k]))
            acc = acc + jnp.dot(picked, panel[pl.ds(start, block), :], preferred_element_type=jnp.float32)
        out_ref[t] = acc


def owner_slot(col, me, per_dev):
    owner, q = col // per_dev, col % per_dev
    dk = (owner % 2) ^ (me % 2)
    dx = ((owner // 2) % 4 - (me // 2) % 4 + 4) % 4
    dy = ((owner // 8) % 2) ^ ((me // 8) % 2)
    dz = ((owner // 16) - (me // 16) + 4) % 4
    half, q2 = q // 2, q % 2
    first = jnp.where(half == 0, dx, dz)
    second = jnp.where(half == 0, dz, dx)
    return (dk * 2 + half) * 64 + ((first * 4 + second) * 2 + dy) * 2 + q2


def spread_kernel(side_ref, cols_ref, count_ref, vals_hbm, grad_ref, keep_hbm, send_hbm, vals, total, sems):
    row_blocks, slot_total, block, _ = vals.shape
    per_panel = grad_ref.shape[1]
    col_blocks = total.shape[0]
    per_dev = col_blocks // 64
    me = side_ref[1]
    load_vals = pltpu.make_async_copy(vals_hbm, vals, sems.at[0])
    load_vals.start()

    def clear(c, carry):
        total[c] = jnp.zeros(total.shape[1:], total.dtype)
        return carry

    lax.fori_loop(0, col_blocks, clear, 0)
    load_vals.wait()
    for t in range(row_blocks):
        live = jnp.clip(count_ref[t], 0, slot_total)
        panel, within = divmod(t, per_panel)
        grad = grad_ref[jnp.where(side_ref[0] == panel, 0, 1), within]

        for k in range(slot_total):
            col = jnp.clip(cols_ref[t, k], 0, col_blocks - 1)
            picked = jnp.where(k < live, vals[t, k], jnp.zeros_like(vals[t, k]))
            contrib = jnp.dot(picked, grad, preferred_element_type=jnp.float32)
            slot = owner_slot(col, me, per_dev)
            total[slot] += contrib
    half = col_blocks // 2
    keep = pltpu.make_async_copy(total.at[pl.ds(0, half)], keep_hbm, sems.at[1])
    send = pltpu.make_async_copy(total.at[pl.ds(half, half)], send_hbm, sems.at[2])
    send.start()
    keep.start()
    send.wait()
    keep.wait()


def aggregate(cols, count, vals, panel):
    row_blocks, slot_total, block, _ = vals.shape
    width = panel.shape[1]
    return pl.pallas_call(
        aggregate_kernel,
        out_shape=jax.ShapeDtypeStruct((row_blocks, block, width), jnp.float32),
        in_specs=[
            pl.BlockSpec(memory_space=pltpu.SMEM),
            pl.BlockSpec(memory_space=pltpu.SMEM),
            pl.BlockSpec(memory_space=pl.ANY),
            pl.BlockSpec(memory_space=pl.ANY),
        ],
        out_specs=pl.BlockSpec(memory_space=pltpu.VMEM),
        scratch_shapes=[
            pltpu.VMEM(vals.shape, vals.dtype),
            pltpu.VMEM(panel.shape, panel.dtype),
            pltpu.SemaphoreType.DMA((2,)),
        ],
        compiler_params=pltpu.CompilerParams(vmem_limit_bytes=VMEM_LIMIT),
        cost_estimate=pl.CostEstimate(
            flops=2 * row_blocks * slot_total * block * block * width,
            bytes_accessed=vals.size * 2 + panel.size * 2 + row_blocks * block * width * 4,
            transcendentals=0,
        ),
    )(cols, count, vals, panel)


def spread(side, cols, count, vals, grad, col_blocks):
    row_blocks, slot_total, block, _ = vals.shape
    width = grad.shape[-1]
    return pl.pallas_call(
        spread_kernel,
        out_shape=[jax.ShapeDtypeStruct((col_blocks // 2, block, width), jnp.float32)] * 2,
        in_specs=[
            pl.BlockSpec(memory_space=pltpu.SMEM),
            pl.BlockSpec(memory_space=pltpu.SMEM),
            pl.BlockSpec(memory_space=pltpu.SMEM),
            pl.BlockSpec(memory_space=pl.ANY),
            pl.BlockSpec(memory_space=pltpu.VMEM),
        ],
        out_specs=[pl.BlockSpec(memory_space=pl.ANY)] * 2,
        scratch_shapes=[
            pltpu.VMEM(vals.shape, vals.dtype),
            pltpu.VMEM((col_blocks, block, width), jnp.float32),
            pltpu.SemaphoreType.DMA((3,)),
        ],
        compiler_params=pltpu.CompilerParams(vmem_limit_bytes=VMEM_LIMIT),
        cost_estimate=pl.CostEstimate(
            flops=2 * row_blocks * slot_total * block * block * width,
            bytes_accessed=vals.size * 2 + grad.size * 2 + col_blocks * block * width * 4,
            transcendentals=0,
        ),
    )(side, cols, count, vals, grad)


def swap(value, axis):
    size = lax.axis_size(axis)
    return lax.ppermute(value, axis, [(i, i ^ 1) for i in range(size)])


def shifted(value, digit, size, shift):
    def dest(r):
        place = (r // digit) % size
        return r + (((place + shift) % size) - place) * digit

    return lax.ppermute(value, "row", [(r, dest(r)) for r in range(64)])


def row_reduce_scatter(keep, send):
    _, block, width = keep.shape
    keep = keep.reshape(2, 4, 16, block, width)
    came = shifted(send, 1, 2, 1).reshape(2, 4, 16, block, width)
    first = [keep[0, s] + came[0, s] for s in range(4)]
    second = [keep[1, s] + came[1, s] for s in range(4)]
    first = (first[0] + sum(shifted(first[s], 2, 4, s) for s in range(1, 4))).reshape(4, 4, block, width)
    second = (second[0] + sum(shifted(second[s], 16, 4, s) for s in range(1, 4))).reshape(4, 4, block, width)
    first = (first[0] + sum(shifted(first[s], 16, 4, s) for s in range(1, 4))).reshape(2, 2, block, width)
    second = (second[0] + sum(shifted(second[s], 2, 4, s) for s in range(1, 4))).reshape(2, 2, block, width)
    first = first[0] + shifted(first[1], 8, 2, 1)
    second = second[0] + shifted(second[1], 8, 2, 1)
    return jnp.concatenate([first, second]).reshape(-1, width)


def all_sum(value, axis):
    size = lax.axis_size(axis)
    step = 1
    while step < size:
        value = value + lax.ppermute(value, axis, [(i, i ^ step) for i in range(size)])
        step *= 2
    return value


def body(features, weight, block_vals, block_cols, block_count, cotangent):
    rows_dev, width = features.shape
    block = block_vals.shape[-1]
    groups = lax.axis_size("grp")
    members = lax.axis_size("row")
    verts = rows_dev * groups * members
    side = lax.axis_index("grp")
    gathered = lax.all_gather(features, "row", axis=0, tiled=True)
    col_blocks = gathered.shape[0] // block
    cols = block_cols[0]
    count = block_count[0]
    vals = block_vals[0]
    flipped, gathered = lax.optimization_barrier((jnp.swapaxes(vals, 2, 3), gathered))

    partial_value = aggregate(cols, count, vals, gathered).reshape(-1, width)
    mine = lax.dynamic_slice_in_dim(partial_value, side * rows_dev, rows_dev)
    theirs = lax.dynamic_slice_in_dim(partial_value, (1 - side) * rows_dev, rows_dev)
    summed = mine + swap(theirs, "grp")
    aggregated = summed.astype(jnp.bfloat16)
    pre = jnp.dot(aggregated, weight, preferred_element_type=jnp.float32)
    activated = jax.nn.silu(pre).astype(jnp.bfloat16)
    pre_grad = (cotangent.astype(jnp.float32) * silu_slope(pre)).astype(jnp.bfloat16)
    local_grad = jnp.dot(aggregated.T, pre_grad, preferred_element_type=jnp.float32)
    own_grad = jnp.dot(pre_grad, weight.T, preferred_element_type=jnp.float32).astype(jnp.bfloat16)
    both_grad = jnp.stack([own_grad, swap(own_grad, "grp")]).reshape(2, -1, block, width)
    weight_grad = all_sum(all_sum(local_grad, "grp"), "row")
    weight_grad, both_grad = lax.optimization_barrier((weight_grad, both_grad))
    weight_grad = weight_grad * (1.0 / math.sqrt(verts))

    where = jnp.stack([side, lax.axis_index("row")]).astype(jnp.int32)
    keep, send = spread(where, cols, count, flipped, both_grad, col_blocks)
    input_grad = row_reduce_scatter(keep, send).astype(jnp.bfloat16)
    return (activated, weight_grad, input_grad)


def solution(mesh):
    placed = (
        P(("grp", "row"), None),
        P(),
        P("grp", "row", None, None, None),
        P("grp", "row", None),
        P("grp", "row"),
        P(("grp", "row"), None),
    )
    return jax.shard_map(
        body,
        mesh=mesh,
        in_specs=placed,
        out_specs=(P(("grp", "row"), None), P(), P(("grp", "row"), None)),
        check_vma=False,
    )
```

```python
import functools
import math

import jax
import jax.numpy as jnp
from jax import lax
from jax.experimental import pallas as pl
from jax.experimental.pallas import tpu as pltpu
from jax.sharding import PartitionSpec as P

VMEM_LIMIT = 60 * 1024 * 1024


def silu_slope(pre):
    sigma = jax.nn.sigmoid(pre)
    return sigma * (1.0 + pre * (1.0 - sigma))


def aggregate_kernel(cols_ref, count_ref, vals_hbm, panel_hbm, out_ref, vals, panel, sems):
    row_blocks, slot_total, block, _ = vals.shape
    col_blocks = panel.shape[0] // block
    load_vals = pltpu.make_async_copy(vals_hbm, vals, sems.at[0])
    load_panel = pltpu.make_async_copy(panel_hbm, panel, sems.at[1])
    load_vals.start()
    load_panel.start()
    load_vals.wait()
    load_panel.wait()
    for t in range(row_blocks):
        live = jnp.clip(count_ref[t], 0, slot_total)

        acc = jnp.zeros(out_ref.shape[1:], jnp.float32)
        for k in range(slot_total):
            col = jnp.clip(cols_ref[t, k], 0, col_blocks - 1)
            start = pl.multiple_of(col * block, block)
            picked = jnp.where(k < live, vals[t, k], jnp.zeros_like(vals[t, k]))
            acc = acc + jnp.dot(picked, panel[pl.ds(start, block), :], preferred_element_type=jnp.float32)
        out_ref[t] = acc


def owner_slot(col, me, per_dev):
    owner, q = col // per_dev, col % per_dev
    dk = (owner % 2) ^ (me % 2)
    dx = ((owner // 2) % 4 - (me // 2) % 4 + 4) % 4
    dy = ((owner // 8) % 2) ^ ((me // 8) % 2)
    dz = ((owner // 16) - (me // 16) + 4) % 4
    half, q2 = q // 2, q % 2
    first = jnp.where(half == 0, dx, dz)
    second = jnp.where(half == 0, dz, dx)
    return (dk * 2 + half) * 64 + ((first * 4 + second) * 2 + dy) * 2 + q2


def spread_kernel(side_ref, cols_ref, count_ref, vals_hbm, grad_ref, keep_hbm, send_hbm, later_hbm, vals, total, sems):
    row_blocks, slot_total, block, _ = vals.shape
    per_panel = grad_ref.shape[1]
    col_blocks = total.shape[0]
    per_dev = col_blocks // 64
    me = side_ref[1]
    load_vals = pltpu.make_async_copy(vals_hbm, vals, sems.at[0])
    load_vals.start()

    def clear(c, carry):
        total[c] = jnp.zeros(total.shape[1:], total.dtype)
        return carry

    lax.fori_loop(0, col_blocks, clear, 0)
    load_vals.wait()
    for t in range(row_blocks):
        live = jnp.clip(count_ref[t], 0, slot_total)
        panel, within = divmod(t, per_panel)
        grad = grad_ref[jnp.where(side_ref[0] == panel, 0, 1), within]

        for k in range(slot_total):
            col = jnp.clip(cols_ref[t, k], 0, col_blocks - 1)
            picked = jnp.where(k < live, vals[t, k], jnp.zeros_like(vals[t, k]))
            contrib = jnp.dot(picked, grad, preferred_element_type=jnp.float32)
            slot = owner_slot(col, me, per_dev)
            total[slot] += contrib
    half = col_blocks // 2
    quarter = half // 2
    keep = pltpu.make_async_copy(total.at[pl.ds(0, half)], keep_hbm, sems.at[1])
    send = pltpu.make_async_copy(total.at[pl.ds(half, quarter)], send_hbm, sems.at[2])
    later = pltpu.make_async_copy(total.at[pl.ds(half + quarter, quarter)], later_hbm, sems.at[3])
    send.start()
    later.start()
    keep.start()
    send.wait()
    later.wait()
    keep.wait()


def aggregate(cols, count, vals, panel):
    row_blocks, slot_total, block, _ = vals.shape
    width = panel.shape[1]
    return pl.pallas_call(
        aggregate_kernel,
        out_shape=jax.ShapeDtypeStruct((row_blocks, block, width), jnp.float32),
        in_specs=[
            pl.BlockSpec(memory_space=pltpu.SMEM),
            pl.BlockSpec(memory_space=pltpu.SMEM),
            pl.BlockSpec(memory_space=pl.ANY),
            pl.BlockSpec(memory_space=pl.ANY),
        ],
        out_specs=pl.BlockSpec(memory_space=pltpu.VMEM),
        scratch_shapes=[
            pltpu.VMEM(vals.shape, vals.dtype),
            pltpu.VMEM(panel.shape, panel.dtype),
            pltpu.SemaphoreType.DMA((2,)),
        ],
        compiler_params=pltpu.CompilerParams(vmem_limit_bytes=VMEM_LIMIT),
        cost_estimate=pl.CostEstimate(
            flops=2 * row_blocks * slot_total * block * block * width,
            bytes_accessed=vals.size * 2 + panel.size * 2 + row_blocks * block * width * 4,
            transcendentals=0,
        ),
    )(cols, count, vals, panel)


def spread(side, cols, count, vals, grad, col_blocks):
    row_blocks, slot_total, block, _ = vals.shape
    width = grad.shape[-1]
    return pl.pallas_call(
        spread_kernel,
        out_shape=[
            jax.ShapeDtypeStruct((col_blocks // 2, block, width), jnp.float32),
            jax.ShapeDtypeStruct((col_blocks // 4, block, width), jnp.float32),
            jax.ShapeDtypeStruct((col_blocks // 4, block, width), jnp.float32),
        ],
        in_specs=[
            pl.BlockSpec(memory_space=pltpu.SMEM),
            pl.BlockSpec(memory_space=pltpu.SMEM),
            pl.BlockSpec(memory_space=pltpu.SMEM),
            pl.BlockSpec(memory_space=pl.ANY),
            pl.BlockSpec(memory_space=pltpu.VMEM),
        ],
        out_specs=[pl.BlockSpec(memory_space=pl.ANY)] * 3,
        scratch_shapes=[
            pltpu.VMEM(vals.shape, vals.dtype),
            pltpu.VMEM((col_blocks, block, width), jnp.float32),
            pltpu.SemaphoreType.DMA((4,)),
        ],
        compiler_params=pltpu.CompilerParams(vmem_limit_bytes=VMEM_LIMIT),
        cost_estimate=pl.CostEstimate(
            flops=2 * row_blocks * slot_total * block * block * width,
            bytes_accessed=vals.size * 2 + grad.size * 2 + col_blocks * block * width * 4,
            transcendentals=0,
        ),
    )(side, cols, count, vals, grad)


def swap(value, axis):
    size = lax.axis_size(axis)
    return lax.ppermute(value, axis, [(i, i ^ 1) for i in range(size)])


def shifted(value, digit, size, shift):
    def dest(r):
        place = (r // digit) % size
        return r + (((place + shift) % size) - place) * digit

    return lax.ppermute(value, "row", [(r, dest(r)) for r in range(64)])


def row_reduce_scatter(keep, send, later):
    _, block, width = keep.shape
    keep = keep.reshape(2, 4, 16, block, width)
    came = shifted(send, 1, 2, 1).reshape(4, 16, block, width)
    first = [keep[0, s] + came[s] for s in range(4)]
    came = shifted(later, 1, 2, 1).reshape(4, 16, block, width)
    second = [keep[1, s] + came[s] for s in range(4)]
    first = (first[0] + sum(shifted(first[s], 2, 4, s) for s in range(1, 4))).reshape(4, 4, block, width)
    second = (second[0] + sum(shifted(second[s], 16, 4, s) for s in range(1, 4))).reshape(4, 4, block, width)
    first = (first[0] + sum(shifted(first[s], 16, 4, s) for s in range(1, 4))).reshape(2, 2, block, width)
    second = (second[0] + sum(shifted(second[s], 2, 4, s) for s in range(1, 4))).reshape(2, 2, block, width)
    first = first[0] + shifted(first[1], 8, 2, 1)
    second = second[0] + shifted(second[1], 8, 2, 1)
    return jnp.concatenate([first, second]).reshape(-1, width)


def all_sum(value, axis):
    size = lax.axis_size(axis)
    step = 1
    while step < size:
        value = value + lax.ppermute(value, axis, [(i, i ^ step) for i in range(size)])
        step *= 2
    return value


def body(features, weight, block_vals, block_cols, block_count, cotangent):
    rows_dev, width = features.shape
    block = block_vals.shape[-1]
    groups = lax.axis_size("grp")
    members = lax.axis_size("row")
    verts = rows_dev * groups * members
    side = lax.axis_index("grp")
    gathered = lax.all_gather(features, "row", axis=0, tiled=True)
    col_blocks = gathered.shape[0] // block
    cols = block_cols[0]
    count = block_count[0]
    vals = block_vals[0]
    flipped, gathered = lax.optimization_barrier((jnp.swapaxes(vals, 2, 3), gathered))

    partial_value = aggregate(cols, count, vals, gathered).reshape(-1, width)
    mine = lax.dynamic_slice_in_dim(partial_value, side * rows_dev, rows_dev)
    theirs = lax.dynamic_slice_in_dim(partial_value, (1 - side) * rows_dev, rows_dev)
    summed = mine + swap(theirs, "grp")
    aggregated = summed.astype(jnp.bfloat16)
    pre = jnp.dot(aggregated, weight, preferred_element_type=jnp.float32)
    activated = jax.nn.silu(pre).astype(jnp.bfloat16)
    pre_grad = (cotangent.astype(jnp.float32) * silu_slope(pre)).astype(jnp.bfloat16)
    local_grad = jnp.dot(aggregated.T, pre_grad, preferred_element_type=jnp.float32)
    own_grad = jnp.dot(pre_grad, weight.T, preferred_element_type=jnp.float32).astype(jnp.bfloat16)
    both_grad = jnp.stack([own_grad, swap(own_grad, "grp")]).reshape(2, -1, block, width)
    weight_grad = all_sum(all_sum(local_grad, "grp"), "row")
    weight_grad, both_grad = lax.optimization_barrier((weight_grad, both_grad))
    weight_grad = weight_grad * (1.0 / math.sqrt(verts))

    where = jnp.stack([side, lax.axis_index("row")]).astype(jnp.int32)
    keep, send, later = spread(where, cols, count, flipped, both_grad, col_blocks)
    input_grad = row_reduce_scatter(keep, send, later).astype(jnp.bfloat16)
    return (activated, weight_grad, input_grad)


def solution(mesh):
    placed = (
        P(("grp", "row"), None),
        P(),
        P("grp", "row", None, None, None),
        P("grp", "row", None),
        P("grp", "row"),
        P(("grp", "row"), None),
    )
    return jax.shard_map(
        body,
        mesh=mesh,
        in_specs=placed,
        out_specs=(P(("grp", "row"), None), P(), P(("grp", "row"), None)),
        check_vma=False,
    )
```

```python
import functools
import math

import jax
import jax.numpy as jnp
from jax import lax
from jax.experimental import pallas as pl
from jax.experimental.pallas import tpu as pltpu
from jax.sharding import PartitionSpec as P

VMEM_LIMIT = 60 * 1024 * 1024


def silu_slope(pre):
    sigma = jax.nn.sigmoid(pre)
    return sigma * (1.0 + pre * (1.0 - sigma))


def aggregate_kernel(cols_ref, count_ref, vals_hbm, panel_hbm, out_ref, vals, panel, sems):
    row_blocks, slot_total, block, _ = vals.shape
    col_blocks = panel.shape[0] // block
    load_vals = pltpu.make_async_copy(vals_hbm, vals, sems.at[0])
    load_panel = pltpu.make_async_copy(panel_hbm, panel, sems.at[1])
    load_vals.start()
    load_panel.start()
    load_vals.wait()
    load_panel.wait()
    for t in range(row_blocks):
        live = jnp.clip(count_ref[t], 0, slot_total)

        acc = jnp.zeros(out_ref.shape[1:], jnp.float32)
        for k in range(slot_total):
            col = jnp.clip(cols_ref[t, k], 0, col_blocks - 1)
            start = pl.multiple_of(col * block, block)
            picked = jnp.where(k < live, vals[t, k], jnp.zeros_like(vals[t, k]))
            acc = acc + jnp.dot(picked, panel[pl.ds(start, block), :], preferred_element_type=jnp.float32)
        out_ref[t] = acc


def owner_slot(col, me, per_dev):
    owner, q = col // per_dev, col % per_dev
    dk = (owner % 2) ^ (me % 2)
    dx = ((owner // 2) % 4 - (me // 2) % 4 + 4) % 4
    dy = ((owner // 8) % 2) ^ ((me // 8) % 2)
    dz = ((owner // 16) - (me // 16) + 4) % 4
    half, q2 = q // 2, q % 2
    first = jnp.where(half == 0, dx, dz)
    second = jnp.where(half == 0, dz, dx)
    return (dk * 2 + half) * 64 + ((first * 4 + second) * 2 + dy) * 2 + q2


def spread_kernel(side_ref, cols_ref, count_ref, vals_hbm, grad_ref, keep_hbm, send_hbm, vals, total, sems):
    row_blocks, slot_total, block, _ = vals.shape
    per_panel = grad_ref.shape[1]
    col_blocks = total.shape[0]
    per_dev = col_blocks // 64
    me = side_ref[1]
    load_vals = pltpu.make_async_copy(vals_hbm, vals, sems.at[0])
    load_vals.start()

    def clear(c, carry):
        total[c] = jnp.zeros(total.shape[1:], total.dtype)
        return carry

    lax.fori_loop(0, col_blocks, clear, 0, unroll=8)
    load_vals.wait()
    for t in range(row_blocks):
        live = jnp.clip(count_ref[t], 0, slot_total)
        panel, within = divmod(t, per_panel)
        grad = grad_ref[jnp.where(side_ref[0] == panel, 0, 1), within]

        for k in range(slot_total):
            col = jnp.clip(cols_ref[t, k], 0, col_blocks - 1)
            picked = jnp.where(k < live, vals[t, k], jnp.zeros_like(vals[t, k]))
            contrib = jnp.dot(picked, grad, preferred_element_type=jnp.float32)
            slot = owner_slot(col, me, per_dev)
            total[slot] += contrib
    half = col_blocks // 2
    keep = pltpu.make_async_copy(total.at[pl.ds(0, half)], keep_hbm, sems.at[1])
    send = pltpu.make_async_copy(total.at[pl.ds(half, half)], send_hbm, sems.at[2])
    send.start()
    keep.start()
    send.wait()
    keep.wait()


def aggregate(cols, count, vals, panel):
    row_blocks, slot_total, block, _ = vals.shape
    width = panel.shape[1]
    return pl.pallas_call(
        aggregate_kernel,
        out_shape=jax.ShapeDtypeStruct((row_blocks, block, width), jnp.float32),
        in_specs=[
            pl.BlockSpec(memory_space=pltpu.SMEM),
            pl.BlockSpec(memory_space=pltpu.SMEM),
            pl.BlockSpec(memory_space=pl.ANY),
            pl.BlockSpec(memory_space=pl.ANY),
        ],
        out_specs=pl.BlockSpec(memory_space=pltpu.VMEM),
        scratch_shapes=[
            pltpu.VMEM(vals.shape, vals.dtype),
            pltpu.VMEM(panel.shape, panel.dtype),
            pltpu.SemaphoreType.DMA((2,)),
        ],
        compiler_params=pltpu.CompilerParams(vmem_limit_bytes=VMEM_LIMIT),
        cost_estimate=pl.CostEstimate(
            flops=2 * row_blocks * slot_total * block * block * width,
            bytes_accessed=vals.size * 2 + panel.size * 2 + row_blocks * block * width * 4,
            transcendentals=0,
        ),
    )(cols, count, vals, panel)


def spread(side, cols, count, vals, grad, col_blocks):
    row_blocks, slot_total, block, _ = vals.shape
    width = grad.shape[-1]
    return pl.pallas_call(
        spread_kernel,
        out_shape=[jax.ShapeDtypeStruct((col_blocks // 2, block, width), jnp.float32)] * 2,
        in_specs=[
            pl.BlockSpec(memory_space=pltpu.SMEM),
            pl.BlockSpec(memory_space=pltpu.SMEM),
            pl.BlockSpec(memory_space=pltpu.SMEM),
            pl.BlockSpec(memory_space=pl.ANY),
            pl.BlockSpec(memory_space=pltpu.VMEM),
        ],
        out_specs=[pl.BlockSpec(memory_space=pl.ANY)] * 2,
        scratch_shapes=[
            pltpu.VMEM(vals.shape, vals.dtype),
            pltpu.VMEM((col_blocks, block, width), jnp.float32),
            pltpu.SemaphoreType.DMA((3,)),
        ],
        compiler_params=pltpu.CompilerParams(vmem_limit_bytes=VMEM_LIMIT),
        cost_estimate=pl.CostEstimate(
            flops=2 * row_blocks * slot_total * block * block * width,
            bytes_accessed=vals.size * 2 + grad.size * 2 + col_blocks * block * width * 4,
            transcendentals=0,
        ),
    )(side, cols, count, vals, grad)


def swap(value, axis):
    size = lax.axis_size(axis)
    return lax.ppermute(value, axis, [(i, i ^ 1) for i in range(size)])


def shifted(value, digit, size, shift):
    def dest(r):
        place = (r // digit) % size
        return r + (((place + shift) % size) - place) * digit

    return lax.ppermute(value, "row", [(r, dest(r)) for r in range(64)])


def row_reduce_scatter(keep, send):
    _, block, width = keep.shape
    keep = keep.reshape(2, 4, 16, block, width)
    came = shifted(send, 1, 2, 1).reshape(2, 4, 16, block, width)
    first = [keep[0, s] + came[0, s] for s in range(4)]
    second = [keep[1, s] + came[1, s] for s in range(4)]
    first = (first[0] + sum(shifted(first[s], 2, 4, s) for s in range(1, 4))).reshape(4, 4, block, width)
    second = (second[0] + sum(shifted(second[s], 16, 4, s) for s in range(1, 4))).reshape(4, 4, block, width)
    first = (first[0] + sum(shifted(first[s], 16, 4, s) for s in range(1, 4))).reshape(2, 2, block, width)
    second = (second[0] + sum(shifted(second[s], 2, 4, s) for s in range(1, 4))).reshape(2, 2, block, width)
    first = first[0] + shifted(first[1], 8, 2, 1)
    second = second[0] + shifted(second[1], 8, 2, 1)
    return jnp.concatenate([first, second]).reshape(-1, width)


def all_sum(value, axis):
    size = lax.axis_size(axis)
    step = 1
    while step < size:
        value = value + lax.ppermute(value, axis, [(i, i ^ step) for i in range(size)])
        step *= 2
    return value


def body(features, weight, block_vals, block_cols, block_count, cotangent):
    rows_dev, width = features.shape
    block = block_vals.shape[-1]
    groups = lax.axis_size("grp")
    members = lax.axis_size("row")
    verts = rows_dev * groups * members
    side = lax.axis_index("grp")
    gathered = lax.all_gather(features, "row", axis=0, tiled=True)
    col_blocks = gathered.shape[0] // block
    cols = block_cols[0]
    count = block_count[0]
    vals = block_vals[0]
    flipped, gathered = lax.optimization_barrier((jnp.swapaxes(vals, 2, 3), gathered))

    partial_value = aggregate(cols, count, vals, gathered).reshape(-1, width)
    mine = lax.dynamic_slice_in_dim(partial_value, side * rows_dev, rows_dev)
    theirs = lax.dynamic_slice_in_dim(partial_value, (1 - side) * rows_dev, rows_dev)
    summed = mine + swap(theirs, "grp")
    aggregated = summed.astype(jnp.bfloat16)
    pre = jnp.dot(aggregated, weight, preferred_element_type=jnp.float32)
    activated = jax.nn.silu(pre).astype(jnp.bfloat16)
    pre_grad = (cotangent.astype(jnp.float32) * silu_slope(pre)).astype(jnp.bfloat16)
    local_grad = jnp.dot(aggregated.T, pre_grad, preferred_element_type=jnp.float32)
    own_grad = jnp.dot(pre_grad, weight.T, preferred_element_type=jnp.float32).astype(jnp.bfloat16)
    both_grad = jnp.stack([own_grad, swap(own_grad, "grp")]).reshape(2, -1, block, width)
    weight_grad = all_sum(all_sum(local_grad, "grp"), "row")
    weight_grad, both_grad = lax.optimization_barrier((weight_grad, both_grad))
    weight_grad = weight_grad * (1.0 / math.sqrt(verts))

    where = jnp.stack([side, lax.axis_index("row")]).astype(jnp.int32)
    keep, send = spread(where, cols, count, flipped, both_grad, col_blocks)
    input_grad = row_reduce_scatter(keep, send).astype(jnp.bfloat16)
    return (activated, weight_grad, input_grad)


def solution(mesh):
    placed = (
        P(("grp", "row"), None),
        P(),
        P("grp", "row", None, None, None),
        P("grp", "row", None),
        P("grp", "row"),
        P(("grp", "row"), None),
    )
    return jax.shard_map(
        body,
        mesh=mesh,
        in_specs=placed,
        out_specs=(P(("grp", "row"), None), P(), P(("grp", "row"), None)),
        check_vma=False,
    )
```

```python
import functools
import math

import jax
import jax.numpy as jnp
from jax import lax
from jax.experimental import pallas as pl
from jax.experimental.pallas import tpu as pltpu
from jax.sharding import PartitionSpec as P

VMEM_LIMIT = 60 * 1024 * 1024


def silu_slope(pre):
    sigma = jax.nn.sigmoid(pre)
    return sigma * (1.0 + pre * (1.0 - sigma))


def aggregate_kernel(cols_ref, count_ref, vals_hbm, panel_hbm, out_ref, vals, panel, sems):
    row_blocks, slot_total, block, _ = vals.shape
    col_blocks = panel.shape[0] // block
    load_vals = pltpu.make_async_copy(vals_hbm, vals, sems.at[0])
    load_panel = pltpu.make_async_copy(panel_hbm, panel, sems.at[1])
    load_vals.start()
    load_panel.start()
    load_vals.wait()
    load_panel.wait()
    for t in range(row_blocks):
        live = jnp.clip(count_ref[t], 0, slot_total)

        acc = jnp.zeros(out_ref.shape[1:], jnp.float32)
        for k in range(slot_total):
            col = jnp.clip(cols_ref[t, k], 0, col_blocks - 1)
            start = pl.multiple_of(col * block, block)
            picked = jnp.where(k < live, vals[t, k], jnp.zeros_like(vals[t, k]))
            acc = acc + jnp.dot(picked, panel[pl.ds(start, block), :], preferred_element_type=jnp.float32)
        out_ref[t] = acc


def owner_slot(col, me, per_dev):
    owner, q = col // per_dev, col % per_dev
    dk = (owner % 2) ^ (me % 2)
    dx = ((owner // 2) % 4 - (me // 2) % 4 + 4) % 4
    dy = ((owner // 8) % 2) ^ ((me // 8) % 2)
    dz = ((owner // 16) - (me // 16) + 4) % 4
    half, q2 = q // 2, q % 2
    first = jnp.where(half == 0, dx, dz)
    second = jnp.where(half == 0, dz, dx)
    return (dk * 2 + half) * 64 + ((first * 4 + second) * 2 + dy) * 2 + q2


def spread_kernel(side_ref, cols_ref, count_ref, vals_hbm, grad_ref, keep_hbm, send_hbm, vals, total, sems):
    row_blocks, slot_total, block, _ = vals.shape
    per_panel = grad_ref.shape[1]
    col_blocks = total.shape[0]
    per_dev = col_blocks // 64
    me = side_ref[1]
    load_vals = pltpu.make_async_copy(vals_hbm, vals, sems.at[0])
    load_vals.start()

    def clear(c, carry):
        total[c] = jnp.zeros(total.shape[1:], total.dtype)
        return carry

    lax.fori_loop(0, col_blocks, clear, 0)
    load_vals.wait()
    for t in range(row_blocks):
        live = jnp.clip(count_ref[t], 0, slot_total)
        panel, within = divmod(t, per_panel)
        grad = grad_ref[jnp.where(side_ref[0] == panel, 0, 1), within]

        for k in range(slot_total):
            col = jnp.clip(cols_ref[t, k], 0, col_blocks - 1)
            picked = jnp.where(k < live, vals[t, k], jnp.zeros_like(vals[t, k]))
            contrib = jnp.dot(picked, grad, preferred_element_type=jnp.float32)
            slot = owner_slot(col, me, per_dev)
            total[slot] += contrib
    half = col_blocks // 2
    keep = pltpu.make_async_copy(total.at[pl.ds(0, half)], keep_hbm, sems.at[1])
    send = pltpu.make_async_copy(total.at[pl.ds(half, half)], send_hbm, sems.at[2])
    send.start()
    keep.start()
    send.wait()
    keep.wait()


def aggregate(cols, count, vals, panel):
    row_blocks, slot_total, block, _ = vals.shape
    width = panel.shape[1]
    return pl.pallas_call(
        aggregate_kernel,
        out_shape=jax.ShapeDtypeStruct((row_blocks, block, width), jnp.float32),
        in_specs=[
            pl.BlockSpec(memory_space=pltpu.SMEM),
            pl.BlockSpec(memory_space=pltpu.SMEM),
            pl.BlockSpec(memory_space=pl.ANY),
            pl.BlockSpec(memory_space=pl.ANY),
        ],
        out_specs=pl.BlockSpec(memory_space=pltpu.VMEM),
        scratch_shapes=[
            pltpu.VMEM(vals.shape, vals.dtype),
            pltpu.VMEM(panel.shape, panel.dtype),
            pltpu.SemaphoreType.DMA((2,)),
        ],
        compiler_params=pltpu.CompilerParams(vmem_limit_bytes=VMEM_LIMIT),
        cost_estimate=pl.CostEstimate(
            flops=2 * row_blocks * slot_total * block * block * width,
            bytes_accessed=vals.size * 2 + panel.size * 2 + row_blocks * block * width * 4,
            transcendentals=0,
        ),
    )(cols, count, vals, panel)


def spread(side, cols, count, vals, grad, col_blocks):
    row_blocks, slot_total, block, _ = vals.shape
    width = grad.shape[-1]
    return pl.pallas_call(
        spread_kernel,
        out_shape=[jax.ShapeDtypeStruct((col_blocks // 2, block, width), jnp.float32)] * 2,
        in_specs=[
            pl.BlockSpec(memory_space=pltpu.SMEM),
            pl.BlockSpec(memory_space=pltpu.SMEM),
            pl.BlockSpec(memory_space=pltpu.SMEM),
            pl.BlockSpec(memory_space=pl.ANY),
            pl.BlockSpec(memory_space=pltpu.VMEM),
        ],
        out_specs=[pl.BlockSpec(memory_space=pl.ANY)] * 2,
        scratch_shapes=[
            pltpu.VMEM(vals.shape, vals.dtype),
            pltpu.VMEM((col_blocks, block, width), jnp.float32),
            pltpu.SemaphoreType.DMA((3,)),
        ],
        compiler_params=pltpu.CompilerParams(vmem_limit_bytes=VMEM_LIMIT),
        cost_estimate=pl.CostEstimate(
            flops=2 * row_blocks * slot_total * block * block * width,
            bytes_accessed=vals.size * 2 + grad.size * 2 + col_blocks * block * width * 4,
            transcendentals=0,
        ),
    )(side, cols, count, vals, grad)


def swap(value, axis):
    size = lax.axis_size(axis)
    return lax.ppermute(value, axis, [(i, i ^ 1) for i in range(size)])


def shifted(value, digit, size, shift):
    def dest(r):
        place = (r // digit) % size
        return r + (((place + shift) % size) - place) * digit

    return lax.ppermute(value, "row", [(r, dest(r)) for r in range(64)])


def row_reduce_scatter(keep, send):
    _, block, width = keep.shape
    keep = keep.reshape(2, 4, 16, block, width)
    came = shifted(send, 1, 2, 1).reshape(2, 4, 16, block, width)
    first = [keep[0, s] + came[0, s] for s in range(4)]
    second = [keep[1, s] + came[1, s] for s in range(4)]
    first = (first[0] + sum(shifted(first[s], 2, 4, s) for s in range(1, 4))).reshape(4, 4, block, width)
    second = (second[0] + sum(shifted(second[s], 16, 4, s) for s in range(1, 4))).reshape(4, 4, block, width)
    first = (first[0] + sum(shifted(first[s], 16, 4, s) for s in range(1, 4))).reshape(2, 2, block, width)
    second = (second[0] + sum(shifted(second[s], 2, 4, s) for s in range(1, 4))).reshape(2, 2, block, width)
    first = first[0] + shifted(first[1], 8, 2, 1)
    second = second[0] + shifted(second[1], 8, 2, 1)
    return jnp.concatenate([first, second]).reshape(-1, width)


def all_sum(value, axis):
    size = lax.axis_size(axis)
    step = 1
    while step < size:
        value = value + lax.ppermute(value, axis, [(i, i ^ step) for i in range(size)])
        step *= 2
    return value


def body(features, weight, block_vals, block_cols, block_count, cotangent):
    rows_dev, width = features.shape
    block = block_vals.shape[-1]
    groups = lax.axis_size("grp")
    members = lax.axis_size("row")
    verts = rows_dev * groups * members
    side = lax.axis_index("grp")
    gathered = lax.all_gather(features, "row", axis=0, tiled=True)
    col_blocks = gathered.shape[0] // block
    cols = block_cols[0]
    count = block_count[0]
    vals = block_vals[0]
    flipped, gathered = lax.optimization_barrier((jnp.swapaxes(vals, 2, 3), gathered))

    partial_value = aggregate(cols, count, vals, gathered).reshape(-1, width)
    mine = lax.dynamic_slice_in_dim(partial_value, side * rows_dev, rows_dev)
    theirs = lax.dynamic_slice_in_dim(partial_value, (1 - side) * rows_dev, rows_dev)
    summed = mine + swap(theirs, "grp")
    aggregated = summed.astype(jnp.bfloat16)
    pre = jnp.dot(aggregated, weight, preferred_element_type=jnp.float32)
    activated = jax.nn.silu(pre).astype(jnp.bfloat16)
    pre_grad = (cotangent.astype(jnp.float32) * silu_slope(pre)).astype(jnp.bfloat16)
    local_grad = jnp.dot(aggregated.T, pre_grad, preferred_element_type=jnp.float32)
    own_grad = jnp.dot(pre_grad, weight.T, preferred_element_type=jnp.float32).astype(jnp.bfloat16)
    both_grad = jnp.stack([own_grad, swap(own_grad, "grp")]).reshape(2, -1, block, width)
    weight_grad = all_sum(local_grad, "row")
    weight_grad, both_grad = lax.optimization_barrier((weight_grad, both_grad))
    weight_grad = (weight_grad + swap(weight_grad, "grp")) * (1.0 / math.sqrt(verts))

    where = jnp.stack([side, lax.axis_index("row")]).astype(jnp.int32)
    keep, send = spread(where, cols, count, flipped, both_grad, col_blocks)
    input_grad = row_reduce_scatter(keep, send).astype(jnp.bfloat16)
    return (activated, weight_grad, input_grad)


def solution(mesh):
    placed = (
        P(("grp", "row"), None),
        P(),
        P("grp", "row", None, None, None),
        P("grp", "row", None),
        P("grp", "row"),
        P(("grp", "row"), None),
    )
    return jax.shard_map(
        body,
        mesh=mesh,
        in_specs=placed,
        out_specs=(P(("grp", "row"), None), P(), P(("grp", "row"), None)),
        check_vma=False,
    )
```
